32 devices in a mesh: dp: 8 (over z, x), fsdp: 4 (over y, core).
Axes of the slice: x: 2, y: 2, z: 4, core: 2. Of those that a mesh axis runs over, the one named last changes fastest.
Arguments:
- dec_hidden: bfloat16 [1024, 4096], P('dp'), may hold values from -18 to 18
- w_query: bfloat16 [4096, 2048], P(None, 'fsdp'), may hold values from -0.01171875 to 0.01171875
- enc_states: bfloat16 [2, 1536, 2048], P(None, 'dp', 'fsdp')
- w_out: bfloat16 [2048, 4096], P('fsdp'), may hold values from -0.5 to 0.5
- norm_gain: float32 [4096], replicated, may hold values from 0.25 to 1.75
- w_vocab: bfloat16 [4096, 16384], P(None, 'fsdp'), may hold values from -1 to 1
- enc_segment: int32 [1536], replicated, may hold values from 0 to 3, as said below
- dec_segment: int32 [1024], P('dp'), may hold values from 0 to 3, as said below
- seg_map: int32 [8, 4], replicated, may hold values from 0 to 31, as said below
- targets: int32 [1024], P('dp'), may hold values from 0 to 16383
- loss_mask: int32 [1024], P('dp'), may hold values from 0 to 1, as said below
Outputs:
- mean_loss: float32 [], replicated
- grad_hidden: bfloat16 [1024, 4096], P('dp', 'fsdp')
- grad_gain: float32 [4096], P('fsdp')
The draws below stay inside these ranges and needn't reach their ends.
Inputs may be any that keep to these rules, and one draw needn't show every extreme that they name: `enc_segment`: each encoder row of 192 tokens holds 4 segments numbered in order, never falling, each nonempty and at most 80 tokens long; one segment of every row is exactly 80 long. `dec_segment`: each decoder row of 128 tokens holds 4 segments numbered in order, never falling, each nonempty and at most 56 tokens long; one segment of every row is exactly 56 long. seg_map[b, j] names the encoder segment (encoder row times 4 plus its number in that row) read by segment j of decoder row b. Every encoder segment is named exactly once. The encoder row read in column j is (b + o_j) mod 8, with offsets o_j that are the same for every decoder row and differ between columns; one of them is 4 and one is 7. The segments of one encoder row go to different decoder rows. `loss_mask`: the first token of every decoder row has mask 1.
All inputs are finite; a program needn't handle non-finite values.
Results may differ from the reference program's by a relative error of at most 0.0086.
Values may be sent and summed in bfloat16 or wider, within the bound.
No kernel may reach another device: no remote copies, remote signals or barrier semaphores. Data moves between devices by JAX's collectives and lax.ppermute only.
A program may use at most 128 MiB of HBM per device.

```python
import math
import jax
import jax.numpy as jnp
import numpy as np
from jax import lax

D = 4096
HEADS = 32
HEAD_DIM = 64
VOCAB = 16384
SEGS = 4
DEC_LEN = 128
ENC_LEN = 192
ENC_MOST = 80
DEC_MOST = 56
N_DP = 8


def segment_lengths(key, total, longest, rows):
    base = (total - longest) // 6
    spare = total - longest - 3 * base
    key_cuts, key_place = jax.random.split(key)
    cuts = jax.random.randint(key_cuts, (rows, 2), 0, spare + 1)
    lower = jnp.min(cuts, 1)
    upper = jnp.max(cuts, 1)
    others = jnp.stack([base + lower, base + upper - lower, base + spare - upper], 1)
    place = jax.random.randint(key_place, (rows,), 0, 4)
    column = jnp.arange(4)[None, :]
    source_col = jnp.clip(column - (column > place[:, None]).astype(jnp.int32), 0, 2)
    picked = jnp.take_along_axis(others, source_col, 1)
    return jnp.where(column == place[:, None], longest, picked)


def segment_ids(lengths, total):
    bounds = jnp.cumsum(lengths, 1)
    position = jnp.arange(total)
    marks = position[None, :, None] >= bounds[:, None, :3]
    return jnp.sum(marks.astype(jnp.int32), 2).reshape(-1).astype(jnp.int32)


def draw_enc_segment(key, part):
    lengths = segment_lengths(jax.random.fold_in(key, 11), ENC_LEN, ENC_MOST, N_DP)
    return segment_ids(lengths, ENC_LEN)


def draw_dec_segment(key, part):
    lengths = segment_lengths(jax.random.fold_in(key, 12), DEC_LEN, DEC_MOST, N_DP)
    return segment_ids(lengths, DEC_LEN)


def draw_seg_map(key, part):
    key_offsets, key_orders = jax.random.split(jax.random.fold_in(key, 13))
    key_first, key_columns = jax.random.split(key_offsets)
    ranking = jax.random.permutation(key_first, N_DP).astype(jnp.int32)
    values_all = jnp.arange(N_DP).astype(jnp.int32)
    fixed_half = N_DP // 2
    fixed_last = N_DP - 1
    excluded = (values_all == fixed_half) | (values_all == fixed_last)
    score = jnp.where(excluded, ranking + N_DP, ranking)
    rest = jnp.argsort(score, stable=True)[:SEGS - 2].astype(jnp.int32)
    base_offsets = jnp.concatenate([jnp.array([fixed_half, fixed_last], jnp.int32), rest])
    offsets = base_offsets[jax.random.permutation(key_columns, SEGS)]
    orders = jax.vmap(lambda single: jax.random.permutation(single, SEGS))(jax.random.split(key_orders, N_DP))
    sender = (jnp.arange(N_DP)[:, None] + offsets[None, :]) % N_DP
    chosen = jnp.take_along_axis(orders[sender], jnp.broadcast_to(jnp.arange(SEGS)[None, :, None], (N_DP, SEGS, 1)), 2)[:, :, 0]
    return (sender * SEGS + chosen).astype(jnp.int32)


def draw_loss_mask(key, part):
    rolls = jax.random.randint(jax.random.fold_in(key, 14), (N_DP, DEC_LEN), 0, 1000)
    limit = 250 + 500 * jnp.arange(N_DP) // max(N_DP - 1, 1)
    ones = (rolls < limit[:, None]).astype(jnp.int32)
    ones = ones.at[:, 0].set(1)
    return ones.reshape(-1)


def draw_enc_states(key, part):
    shape = (2, N_DP * ENC_LEN, HEADS * HEAD_DIM)
    base_key = jax.random.fold_in(jax.random.fold_in(key, 15), 0)
    values = jax.random.normal(base_key, shape, jnp.float32)
    return jnp.clip(values, -6.0, 6.0).astype(jnp.bfloat16)


def draw_dec_hidden(key, part):
    shape = (N_DP * DEC_LEN, D)
    noise = jnp.clip(jax.random.normal(jax.random.fold_in(key, 22), shape, jnp.float32), -6.0, 6.0)
    return noise.astype(jnp.bfloat16)


def draw_w_vocab(key, part):
    shape = (D, VOCAB)
    noise = jnp.clip(jax.random.normal(jax.random.fold_in(key, 23), shape, jnp.float32), -6.0, 6.0) * (D // 9) ** (-0.5)
    return noise.astype(jnp.bfloat16)


def set_ends(entries, own_key, low, largest):
    spot = [jax.random.randint(jax.random.fold_in(own_key, axis), (), 0, length) for axis, length in enumerate(entries.shape)]
    widest = entries.shape.index(max(entries.shape))
    next_to = spot[:widest] + [(spot[widest] + 1) % entries.shape[widest]] + spot[widest + 1:]
    return entries.at[tuple(spot)].set(low).at[tuple(next_to)].set(largest)


def level_of(own_key, shape, shards, smallest, largest):
    loudness, own = 1.0, jax.random.fold_in(own_key, 6)
    for axis_at, blocks in shards:
        draws = jnp.exp(jax.random.uniform(jax.random.fold_in(own, axis_at), (blocks,), jnp.float32, smallest / len(shards), largest / len(shards)))
        loudness = loudness * jnp.repeat(draws, shape[axis_at] // blocks).reshape([-1 if axis == axis_at else 1 for axis in range(len(shape))])
    return loudness


def cumulative_ranks(number_of, slope):
    loads = [(1 << 20) // math.isqrt(standing ** slope) + 1 for standing in range(1, number_of + 1)]
    scale = 1 + sum(loads) // (1 << 30)
    return np.cumsum(np.array([max(1, weight // scale) for weight in loads]))


def skewed_ids(own_key, dims, count, skew):
    table = cumulative_ranks(count, skew)
    lot = jax.random.randint(jax.random.fold_in(own_key, 1), dims, 0, int(table[count - 1]))
    grade = jnp.searchsorted(jnp.asarray(table, jnp.int32), lot, side="right")
    return jax.random.permutation(jax.random.fold_in(own_key, 2), count)[grade].astype(jnp.int32)


def bell_draw(rng, extent, scale, most, pieces=(), held_as=jnp.bfloat16):
    gain = level_of(rng, extent, pieces, -0.22, 0.18) if pieces else 1.0
    result = jax.random.normal(rng, extent, jnp.float32) * scale * gain
    return jnp.minimum(jnp.maximum(result, -most), most).astype(held_as)


def setup_inputs(seed: int = 0) -> dict:
    keys = jax.random.split(jax.random.key(seed), 12)
    dec_hidden = draw_dec_hidden(jax.random.fold_in(keys[11], 71), 0)
    w_query = bell_draw(keys[1], (D, HEADS * HEAD_DIM), (D * HEAD_DIM) ** -0.5, 0.01171875, ((1, 4),))
    enc_states = draw_enc_states(jax.random.fold_in(keys[11], 71), 0)
    w_out = bell_draw(keys[3], (HEADS * HEAD_DIM, D), (HEADS * HEAD_DIM // 16) ** -0.5, 0.5, ((0, 4),))
    norm_gain = jnp.clip(1.0 + 0.15 * jax.random.normal(keys[4], (D,), jnp.float32), 0.25, 1.75)
    w_vocab = draw_w_vocab(jax.random.fold_in(keys[11], 71), 0)
    enc_segment = draw_enc_segment(jax.random.fold_in(keys[11], 71), 0)
    dec_segment = draw_dec_segment(jax.random.fold_in(keys[11], 71), 0)
    seg_map = draw_seg_map(jax.random.fold_in(keys[11], 71), 0)
    targets = set_ends(skewed_ids(keys[9], (N_DP * DEC_LEN,), VOCAB, 2), jax.random.fold_in(keys[9], 3), 0, VOCAB - 1).astype(jnp.int32)
    loss_mask = draw_loss_mask(jax.random.fold_in(keys[11], 71), 0)
    return {"dec_hidden": dec_hidden, "w_query": w_query, "enc_states": enc_states, "w_out": w_out, "norm_gain": norm_gain, "w_vocab": w_vocab, "enc_segment": enc_segment, "dec_segment": dec_segment, "seg_map": seg_map, "targets": targets, "loss_mask": loss_mask}


def reference(dec_hidden, w_query, enc_states, w_out, norm_gain, w_vocab, enc_segment, dec_segment, seg_map, targets, loss_mask):
    enc_ids = (jnp.arange(N_DP * ENC_LEN) // ENC_LEN).astype(jnp.int32) * SEGS + enc_segment

    def one_row(row_index):
        row_start = (row_index * DEC_LEN).astype(jnp.int32)
        hidden_in = lax.dynamic_slice_in_dim(dec_hidden, row_start, DEC_LEN, 0)
        segment_here = lax.dynamic_slice_in_dim(dec_segment, row_start, DEC_LEN, 0)
        target_here = lax.dynamic_slice_in_dim(targets, row_start, DEC_LEN, 0)
        mask_here = lax.dynamic_slice_in_dim(loss_mask, row_start, DEC_LEN, 0).astype(jnp.float32)
        map_row = lax.dynamic_index_in_dim(seg_map, row_index, 0, keepdims=False)
        sources = jnp.take(map_row, segment_here)
        blocks = []
        block_ids = []
        for column in range(SEGS):
            enc_start = (map_row[column] // SEGS * ENC_LEN).astype(jnp.int32)
            blocks.append(lax.dynamic_slice_in_dim(enc_states, enc_start, ENC_LEN, 1))
            block_ids.append(lax.dynamic_slice_in_dim(enc_ids, enc_start, ENC_LEN, 0))
        gathered = jnp.concatenate(blocks, 1)
        key_ids = jnp.concatenate(block_ids, 0)
        query_proj = jnp.dot(hidden_in, w_query, preferred_element_type=jnp.float32).astype(jnp.bfloat16)
        queries = lax.optimization_barrier(query_proj).astype(jnp.float32).reshape(DEC_LEN, HEADS, HEAD_DIM)
        keys_all = gathered[0].astype(jnp.float32).reshape(SEGS * ENC_LEN, HEADS, HEAD_DIM)
        values_all = gathered[1].astype(jnp.float32).reshape(SEGS * ENC_LEN, HEADS, HEAD_DIM)
        scores = jnp.einsum('ihd,jhd->hij', queries, keys_all)
        allowed = (sources[:, None] == key_ids[None, :])[None]
        weights = jax.nn.softmax(jnp.where(allowed, scores, jnp.float32(-1e+30)), axis=-1)
        attended = jnp.einsum('hij,jhd->ihd', weights, values_all).reshape(DEC_LEN, HEADS * HEAD_DIM).astype(jnp.bfloat16)
        summed = hidden_in.astype(jnp.float32) + jnp.dot(attended, w_out, preferred_element_type=jnp.float32)
        inv_root = lax.rsqrt(lax.optimization_barrier(jnp.mean(summed * summed, 1)) + 1e-06)
        unit = summed * inv_root[:, None]
        normed = (unit * norm_gain).astype(jnp.bfloat16)
        logits = jnp.dot(normed, w_vocab, preferred_element_type=jnp.float32)
        row_top = lax.optimization_barrier(jnp.max(logits, 1))
        log_total = row_top + jnp.log(lax.optimization_barrier(jnp.sum(jnp.exp(logits - row_top[:, None]), 1)))
        picked = jnp.arange(VOCAB)[None, :] == target_here[:, None]
        target_logit = lax.optimization_barrier(jnp.sum(jnp.where(picked, logits, 0.0), 1))
        token_loss = log_total - target_logit
        grad_logits = (mask_here[:, None] * (jnp.exp(logits - log_total[:, None]) - picked.astype(jnp.float32))).astype(jnp.bfloat16)
        grad_normed = lax.dot_general(grad_logits, w_vocab, (((1,), (1,)), ((), ())), preferred_element_type=jnp.float32)
        gain_part = lax.optimization_barrier(jnp.sum(grad_normed * unit, 0))
        grad_unit = grad_normed * norm_gain
        inner_mean = lax.optimization_barrier(jnp.mean(grad_unit * unit, 1))
        grad_summed = inv_root[:, None] * (grad_unit - unit * inner_mean[:, None])
        return (jnp.sum(mask_here), jnp.sum(mask_here * token_loss), gain_part, grad_summed)
    counts, totals, gain_parts, grads = lax.map(one_row, jnp.arange(N_DP).astype(jnp.int32))
    count = jnp.sum(counts)
    mean_loss = jnp.sum(totals) / count
    grad_gain = lax.optimization_barrier(jnp.sum(gain_parts, 0)) / count
    grad_hidden = (grads.reshape(N_DP * DEC_LEN, D) / count).astype(jnp.bfloat16)
    return (mean_loss, grad_hidden, grad_gain)
```

```python
import jax
import jax.numpy as jnp
from jax import lax
from jax.sharding import PartitionSpec as P

HEAD_DIM = 64
ENC_MOST = 80


def is_power_of_two(n):
    return n & (n - 1) == 0


def exchange(x, axis, bit):
    size = lax.axis_size(axis)
    return lax.ppermute(x, axis, [(i, i ^ (1 << bit)) for i in range(size)])


def scatter_sum(x, axis, dim):
    size = lax.axis_size(axis)
    if not is_power_of_two(size):
        return lax.psum_scatter(x, axis, scatter_dimension=dim, tiled=True)
    me = lax.axis_index(axis)
    head, width, tail = x.shape[:dim], x.shape[dim] // size, x.shape[dim + 1 :]
    cur = x
    chunks, bit = size, 0
    while chunks > 1:
        cur = cur.reshape(head + (chunks // 2, 2, width) + tail)
        side = (me >> bit) & 1
        keep = lax.dynamic_index_in_dim(cur, side, dim + 1, keepdims=False)
        send = lax.dynamic_index_in_dim(cur, 1 - side, dim + 1, keepdims=False)
        cur = keep + exchange(send, axis, bit)
        chunks //= 2
        bit += 1
    return cur.reshape(head + (width,) + tail)


def gather_all(x, axis, dim):
    size = lax.axis_size(axis)
    if not is_power_of_two(size):
        return lax.all_gather(x, axis, axis=dim, tiled=True)
    me = lax.axis_index(axis)
    head, width, tail = x.shape[:dim], x.shape[dim], x.shape[dim + 1 :]
    cur = x.reshape(head + (1, width) + tail)
    chunks = 1
    bit = size.bit_length() - 2
    while bit >= 0:
        got = exchange(cur, axis, bit)
        low = (me >> bit) & 1 == 0
        first = jnp.where(low, cur, got)
        second = jnp.where(low, got, cur)
        cur = jnp.stack([first, second], dim + 1).reshape(head + (chunks * 2, width) + tail)
        chunks *= 2
        bit -= 1
    return cur.reshape(head + (chunks * width,) + tail)


def sum_all(x, axis):
    size = lax.axis_size(axis)
    if not is_power_of_two(size):
        return lax.psum(x, axis)
    for bit in range(size.bit_length() - 1):
        x = x + exchange(x, axis, bit)
    return x


def merge_totals(first_set, second_set):
    larger = jnp.maximum(first_set[0], second_set[0])
    combined = first_set[1] * jnp.exp(first_set[0] - larger) + second_set[1] * jnp.exp(
        second_set[0] - larger
    )
    return jnp.stack([larger, combined, first_set[2] + second_set[2]])


def merge_all(stats, axis):
    size = lax.axis_size(axis)
    if is_power_of_two(size):
        for bit in range(size.bit_length() - 1):
            stats = merge_totals(stats, exchange(stats, axis, bit))
        return stats
    everything = lax.all_gather(stats, axis)
    return lax.fori_loop(1, size, lambda k, so_far: merge_totals(so_far, everything[k]), everything[0])


def body(
    dec_hidden,
    w_query,
    enc_states,
    w_out,
    norm_gain,
    w_vocab,
    enc_segment,
    dec_segment,
    seg_map,
    targets,
    loss_mask,
):
    dp_index = lax.axis_index("dp")
    fsdp_index = lax.axis_index("fsdp")
    dp_count = lax.axis_size("dp")
    dec_len, width = dec_hidden.shape
    enc_len = enc_states.shape[1]
    heads_here = w_query.shape[1] // HEAD_DIM
    segments = seg_map.shape[1]
    feature_count = width // lax.axis_size("fsdp")
    vocab_here = w_vocab.shape[1]
    window = min(ENC_MOST, enc_len)

    map_row = lax.dynamic_index_in_dim(seg_map, dp_index, 0, keepdims=False)
    segment_picks = dec_segment[:, None] == jnp.arange(segments)[None, :]
    sources = jnp.sum(jnp.where(segment_picks, map_row[None, :], 0), 1)

    offsets = (seg_map[0] // segments) % dp_count
    column_hits = offsets[None, :] == jnp.arange(dp_count)[:, None]
    shift_used = jnp.any(column_hits, 1)
    shift_column = jnp.argmax(column_hits, 1)
    enc_rows = enc_segment.reshape(dp_count, enc_len)
    seg_starts = jnp.sum(enc_rows[:, None, :] < jnp.arange(segments)[None, :, None], 2)
    win_starts = jnp.clip(seg_starts, 0, enc_len - window)
    global_ids = jnp.arange(dp_count * enc_len) // enc_len * segments + enc_segment

    key_blocks = []
    id_blocks = []
    for shift in range(dp_count):
        column = shift_column[shift]
        reader = (dp_index - shift) % dp_count
        send_segment = seg_map[reader, column] % segments
        send_start = win_starts[dp_index, send_segment]
        block = lax.dynamic_slice_in_dim(enc_states, send_start, window, 1)
        if shift:
            block = lax.ppermute(
                block, "dp", [(i, (i - shift) % dp_count) for i in range(dp_count)]
            )
        owner = (dp_index + shift) % dp_count
        recv_segment = map_row[column] % segments
        recv_start = win_starts[owner, recv_segment]
        ids = lax.dynamic_slice_in_dim(global_ids, owner * enc_len + recv_start, window, 0)
        key_blocks.append(block)
        id_blocks.append(jnp.where(shift_used[shift], ids, -1))
    gathered = jnp.concatenate(key_blocks, 1)
    key_ids = jnp.concatenate(id_blocks, 0)
    key_count = gathered.shape[1]

    query_proj = jnp.dot(dec_hidden, w_query, preferred_element_type=jnp.float32).astype(
        jnp.bfloat16
    )
    queries = lax.optimization_barrier(query_proj).reshape(dec_len, heads_here, HEAD_DIM)
    keys_all = gathered[0].reshape(key_count, heads_here, HEAD_DIM)
    values_all = gathered[1].astype(jnp.float32).reshape(key_count, heads_here, HEAD_DIM)
    scores = jnp.einsum(
        "ihd,jhd->hij", queries, keys_all, preferred_element_type=jnp.float32
    )
    allowed = (sources[:, None] == key_ids[None, :])[None]
    top = jnp.max(jnp.where(allowed, scores, jnp.float32(-1e30)), 2)
    weights = jnp.where(allowed, jnp.exp(scores - top[:, :, None]), 0.0)
    run_sum = jnp.sum(weights, 2)
    run_acc = jnp.einsum("hij,jhd->hid", weights, values_all)
    attended = (
        (run_acc / run_sum[:, :, None])
        .transpose(1, 0, 2)
        .reshape(dec_len, heads_here * HEAD_DIM)
        .astype(jnp.bfloat16)
    )

    feature_start = fsdp_index * feature_count
    gain_part = lax.dynamic_slice_in_dim(norm_gain, feature_start, feature_count, 0)
    hidden_part = lax.dynamic_slice_in_dim(dec_hidden, feature_start, feature_count, 1)
    summed_part = scatter_sum(
        jnp.dot(attended, w_out, preferred_element_type=jnp.float32), "fsdp", 1
    ) + hidden_part.astype(jnp.float32)
    summed_full = gather_all(summed_part, "fsdp", 1)
    inv_root = lax.rsqrt(jnp.sum(summed_full * summed_full, 1) / width + 1e-06)
    unit_full = summed_full * inv_root[:, None]
    normed_full = (unit_full * norm_gain).astype(jnp.bfloat16)
    logits = jnp.dot(normed_full, w_vocab, preferred_element_type=jnp.float32)
    unit_part = summed_part * inv_root[:, None]
    local_target = targets - fsdp_index * vocab_here
    picked = jnp.arange(vocab_here)[None, :] == local_target[:, None]
    local_top = jnp.max(logits, 1)
    local_total = jnp.sum(jnp.exp(logits - local_top[:, None]), 1)
    local_pick = jnp.sum(jnp.where(picked, logits, 0.0), 1)
    row_top, row_total, target_logit = merge_all(
        jnp.stack([local_top, local_total, local_pick]), "fsdp"
    )
    log_total = row_top + jnp.log(row_total)
    mask_float = loss_mask.astype(jnp.float32)
    grad_logits = (
        mask_float[:, None] * (jnp.exp(logits - log_total[:, None]) - picked.astype(jnp.float32))
    ).astype(jnp.bfloat16)
    grad_normed = scatter_sum(
        lax.dot_general(
            w_vocab, grad_logits, (((1,), (1,)), ((), ())), preferred_element_type=jnp.float32
        ),
        "fsdp",
        0,
    ).T
    grad_unit = grad_normed * gain_part
    inner_total = sum_all(jnp.sum(grad_unit * unit_part, 1), "fsdp")
    grad_summed = inv_root[:, None] * (grad_unit - unit_part * (inner_total / width)[:, None])
    gain_local = jnp.sum(grad_normed * unit_part, 0)
    packed = jnp.concatenate(
        [jnp.stack([jnp.sum(mask_float), jnp.sum(mask_float * (log_total - target_logit))]), gain_local]
    )
    packed = sum_all(packed, "dp")
    token_count, loss_total, gain_total = packed[0], packed[1], packed[2:]
    return (
        loss_total / token_count,
        (grad_summed / token_count).astype(jnp.bfloat16),
        gain_total / token_count,
    )


def solution(mesh):
    in_specs = (
        P("dp", None),
        P(None, "fsdp"),
        P(None, "dp", "fsdp"),
        P("fsdp", None),
        P(),
        P(None, "fsdp"),
        P(),
        P("dp"),
        P(),
        P("dp"),
        P("dp"),
    )
    out_specs = (P(), P("dp", "fsdp"), P("fsdp"))
    return jax.shard_map(body, mesh=mesh, in_specs=in_specs, out_specs=out_specs, check_vma=False)
```

```python
import jax
import jax.numpy as jnp
from jax import lax
from jax.sharding import PartitionSpec as P

HEAD_DIM = 64
ENC_MOST = 80


def is_power_of_two(n):
    return n & (n - 1) == 0


def exchange(x, axis, bit):
    size = lax.axis_size(axis)
    return lax.ppermute(x, axis, [(i, i ^ (1 << bit)) for i in range(size)])


def scatter_bits(x, axis, dim, levels):
    me = lax.axis_index(axis)
    chunks = 1 << levels
    head, width, tail = x.shape[:dim], x.shape[dim] // chunks, x.shape[dim + 1 :]
    cur = x
    bit = 0
    while chunks > 1:
        cur = cur.reshape(head + (chunks // 2, 2, width) + tail)
        side = (me >> bit) & 1
        keep = lax.dynamic_index_in_dim(cur, side, dim + 1, keepdims=False)
        send = lax.dynamic_index_in_dim(cur, 1 - side, dim + 1, keepdims=False)
        cur = keep + exchange(send, axis, bit)
        chunks //= 2
        bit += 1
    return cur.reshape(head + (width,) + tail)


def gather_bits(x, axis, dim, levels):
    me = lax.axis_index(axis)
    head, width, tail = x.shape[:dim], x.shape[dim], x.shape[dim + 1 :]
    cur = x.reshape(head + (1, width) + tail)
    chunks = 1
    for bit in range(levels):
        got = exchange(cur, axis, bit)
        low = (me >> bit) & 1 == 0
        first = jnp.where(low, cur, got)
        second = jnp.where(low, got, cur)
        cur = jnp.stack([first, second], dim).reshape(head + (chunks * 2, width) + tail)
        chunks *= 2
    return cur.reshape(head + (chunks * width,) + tail)


def sum_all(x, axis):
    size = lax.axis_size(axis)
    if not is_power_of_two(size):
        return lax.psum(x, axis)
    for bit in range(size.bit_length() - 1):
        x = x + exchange(x, axis, bit)
    return x


def merge_totals(first_set, second_set):
    larger = jnp.maximum(first_set[0], second_set[0])
    combined = first_set[1] * jnp.exp(first_set[0] - larger) + second_set[1] * jnp.exp(
        second_set[0] - larger
    )
    return jnp.stack([larger, combined, first_set[2] + second_set[2]])


def merge_all(stats, axis):
    size = lax.axis_size(axis)
    if is_power_of_two(size):
        for bit in range(size.bit_length() - 1):
            stats = merge_totals(stats, exchange(stats, axis, bit))
        return stats
    everything = lax.all_gather(stats, axis)
    return lax.fori_loop(1, size, lambda k, so_far: merge_totals(so_far, everything[k]), everything[0])


def body(
    dec_hidden,
    w_query,
    enc_states,
    w_out,
    norm_gain,
    w_vocab,
    enc_segment,
    dec_segment,
    seg_map,
    targets,
    loss_mask,
):
    dp_index = lax.axis_index("dp")
    fsdp_index = lax.axis_index("fsdp")
    dp_count = lax.axis_size("dp")
    fsdp_count = lax.axis_size("fsdp")
    dec_len, width = dec_hidden.shape
    enc_len = enc_states.shape[1]
    heads_here = w_query.shape[1] // HEAD_DIM
    segments = seg_map.shape[1]
    feature_count = width // fsdp_count
    vocab_here = w_vocab.shape[1]
    window = min(ENC_MOST, enc_len)
    split_fsdp = is_power_of_two(fsdp_count) and fsdp_count > 1
    levels = fsdp_count.bit_length() - 1

    rows = jnp.arange(dp_count)
    seg_ids = jnp.arange(segments)
    map_row = jnp.sum(jnp.where((rows == dp_index)[:, None], seg_map, 0), 0)
    sources = jnp.sum(
        jnp.where(dec_segment[:, None] == seg_ids[None, :], map_row[None, :], 0), 1
    )
    offsets = (seg_map[0] // segments) % dp_count
    hits = offsets[None, :] == rows[:, None]
    used = jnp.any(hits, 1)
    enc_rows = enc_segment.reshape(dp_count, enc_len)
    all_starts = jnp.sum(enc_rows[:, None, :] < seg_ids[None, :, None], 2)
    reader_hot = ((dp_index - rows) % dp_count)[:, None] == rows[None, :]
    reader_maps = jnp.sum(jnp.where(reader_hot[:, :, None], seg_map[None], 0), 1)
    send_seg = jnp.sum(jnp.where(hits, reader_maps, 0), 1) % segments
    my_starts = jnp.sum(jnp.where((rows == dp_index)[:, None], all_starts, 0), 0)
    send_start = jnp.clip(
        jnp.sum(jnp.where(send_seg[:, None] == seg_ids[None, :], my_starts[None, :], 0), 1),
        0,
        enc_len - window,
    )
    token_at = jnp.arange(enc_len)[None, None, :]
    send_pos = send_start[:, None] + jnp.arange(window)[None, :]
    pick = (token_at == send_pos[:, :, None]).astype(jnp.bfloat16)
    windows = jnp.einsum(
        "str,crf->sctf", pick, enc_states, preferred_element_type=jnp.float32
    ).astype(jnp.bfloat16)
    owner_hot = ((dp_index + rows) % dp_count)[:, None] == rows[None, :]
    owner_rows = jnp.sum(jnp.where(owner_hot[:, :, None], enc_rows[None], 0), 1)
    owner_starts = jnp.sum(jnp.where(owner_hot[:, :, None], all_starts[None], 0), 1)
    served = jnp.sum(jnp.where(hits, map_row[None, :], 0), 1)
    served_local = served % segments
    recv_start = jnp.clip(
        jnp.sum(jnp.where(served_local[:, None] == seg_ids[None, :], owner_starts, 0), 1),
        0,
        enc_len - window,
    )
    recv_pos = recv_start[:, None] + jnp.arange(window)[None, :]
    seg_at = jnp.sum(jnp.where(token_at == recv_pos[:, :, None], owner_rows[:, None, :], 0), 2)
    key_ids = jnp.where(used[:, None] & (seg_at == served_local[:, None]), served[:, None], -1)

    query_proj = jnp.dot(dec_hidden, w_query, preferred_element_type=jnp.float32).astype(
        jnp.bfloat16
    )
    queries = lax.optimization_barrier(query_proj).reshape(dec_len, heads_here, HEAD_DIM)
    run_sum = jnp.zeros((heads_here, dec_len), jnp.float32)
    run_acc = jnp.zeros((heads_here, dec_len, HEAD_DIM), jnp.float32)
    for shift in range(dp_count):
        block = windows[shift]
        if shift:
            block = lax.ppermute(
                block, "dp", [(i, (i - shift) % dp_count) for i in range(dp_count)]
            )
        keys_here = block[0].reshape(window, heads_here, HEAD_DIM)
        values_here = block[1].astype(jnp.float32).reshape(window, heads_here, HEAD_DIM)
        scores = jnp.einsum(
            "ihd,jhd->hij", queries, keys_here, preferred_element_type=jnp.float32
        )
        allowed = (sources[:, None] == key_ids[shift][None, :])[None]
        top = jnp.max(jnp.where(allowed, scores, jnp.float32(-1e30)), 2)
        weights = jnp.where(allowed, jnp.exp(scores - top[:, :, None]), 0.0)
        run_sum = run_sum + jnp.sum(weights, 2)
        run_acc = run_acc + jnp.einsum("hij,jhd->hid", weights, values_here)
    attended = (
        (run_acc / run_sum[:, :, None])
        .transpose(1, 0, 2)
        .reshape(dec_len, heads_here * HEAD_DIM)
        .astype(jnp.bfloat16)
    )

    feature_start = fsdp_index * feature_count
    gain_part = lax.dynamic_slice_in_dim(norm_gain, feature_start, feature_count, 0)
    hidden_part = lax.dynamic_slice_in_dim(dec_hidden, feature_start, feature_count, 1)
    projected = jnp.dot(attended, w_out, preferred_element_type=jnp.float32)
    if split_fsdp:
        projected = scatter_bits(projected, "fsdp", 1, levels)
    else:
        projected = lax.psum_scatter(projected, "fsdp", scatter_dimension=1, tiled=True)
    summed_part = projected + hidden_part.astype(jnp.float32)
    square_total = sum_all(jnp.sum(summed_part * summed_part, 1), "fsdp")
    inv_root = lax.rsqrt(square_total / width + 1e-06)
    unit_part = summed_part * inv_root[:, None]
    normed_part = (unit_part * gain_part).astype(jnp.bfloat16)
    if split_fsdp:
        half = width // 2
        top_side = (fsdp_index >> (levels - 1)) & 1
        near_rows = lax.dynamic_slice_in_dim(w_vocab, top_side * half, half, 0)
        far_rows = lax.dynamic_slice_in_dim(w_vocab, (1 - top_side) * half, half, 0)
        near_normed = gather_bits(normed_part, "fsdp", 1, levels - 1)
        far_normed = exchange(near_normed, "fsdp", levels - 1)
        logits = jnp.dot(near_normed, near_rows, preferred_element_type=jnp.float32) + jnp.dot(
            far_normed, far_rows, preferred_element_type=jnp.float32
        )
    else:
        normed_full = lax.all_gather(normed_part, "fsdp", axis=1, tiled=True)
        logits = jnp.dot(normed_full, w_vocab, preferred_element_type=jnp.float32)
    local_target = targets - fsdp_index * vocab_here
    picked = jnp.arange(vocab_here)[None, :] == local_target[:, None]
    local_top = jnp.max(logits, 1)
    local_total = jnp.sum(jnp.exp(logits - local_top[:, None]), 1)
    local_pick = jnp.sum(jnp.where(picked, logits, 0.0), 1)
    row_top, row_total, target_logit = merge_all(
        jnp.stack([local_top, local_total, local_pick]), "fsdp"
    )
    log_total = row_top + jnp.log(row_total)
    mask_float = loss_mask.astype(jnp.float32)
    grad_logits = (
        mask_float[:, None] * (jnp.exp(logits - log_total[:, None]) - picked.astype(jnp.float32))
    ).astype(jnp.bfloat16)
    contract = (((1,), (1,)), ((), ()))
    if split_fsdp:
        far_grad = lax.dot_general(
            far_rows, grad_logits, contract, preferred_element_type=jnp.float32
        )
        far_grad = exchange(scatter_bits(far_grad, "fsdp", 0, levels - 1), "fsdp", levels - 1)
        near_grad = lax.dot_general(
            near_rows, grad_logits, contract, preferred_element_type=jnp.float32
        )
        grad_normed = (scatter_bits(near_grad, "fsdp", 0, levels - 1) + far_grad).T
    else:
        grad_normed = lax.psum_scatter(
            lax.dot_general(w_vocab, grad_logits, contract, preferred_element_type=jnp.float32),
            "fsdp",
            scatter_dimension=0,
            tiled=True,
        ).T
    grad_unit = grad_normed * gain_part
    inner_total = sum_all(jnp.sum(grad_unit * unit_part, 1), "fsdp")
    grad_summed = inv_root[:, None] * (grad_unit - unit_part * (inner_total / width)[:, None])
    gain_local = jnp.sum(grad_normed * unit_part, 0)
    packed = jnp.concatenate(
        [jnp.stack([jnp.sum(mask_float), jnp.sum(mask_float * (log_total - target_logit))]), gain_local]
    )
    packed = sum_all(packed, "dp")
    token_count, loss_total, gain_total = packed[0], packed[1], packed[2:]
    return (
        loss_total / token_count,
        (grad_summed / token_count).astype(jnp.bfloat16),
        gain_total / token_count,
    )


def solution(mesh):
    in_specs = (
        P("dp", None),
        P(None, "fsdp"),
        P(None, "dp", "fsdp"),
        P("fsdp", None),
        P(),
        P(None, "fsdp"),
        P(),
        P("dp"),
        P(),
        P("dp"),
        P("dp"),
    )
    out_specs = (P(), P("dp", "fsdp"), P("fsdp"))
    return jax.shard_map(body, mesh=mesh, in_specs=in_specs, out_specs=out_specs, check_vma=False)
```

```python
import jax
import jax.numpy as jnp
from jax import lax
from jax.sharding import PartitionSpec as P

HEAD_DIM = 64
ENC_MOST = 80


def is_power_of_two(n):
    return n & (n - 1) == 0


def exchange(x, axis, bit):
    size = lax.axis_size(axis)
    return lax.ppermute(x, axis, [(i, i ^ (1 << bit)) for i in range(size)])


def scatter_bits(x, axis, dim, levels, last_wire=None):
    me = lax.axis_index(axis)
    chunks = 1 << levels
    head, width, tail = x.shape[:dim], x.shape[dim] // chunks, x.shape[dim + 1 :]
    cur = x
    bit = 0
    while chunks > 1:
        cur = cur.reshape(head + (chunks // 2, 2, width) + tail)
        side = (me >> bit) & 1
        keep = lax.dynamic_index_in_dim(cur, side, dim + 1, keepdims=False)
        send = lax.dynamic_index_in_dim(cur, 1 - side, dim + 1, keepdims=False)
        if last_wire is not None and chunks == 2:
            cur = keep + exchange(send.astype(last_wire), axis, bit).astype(keep.dtype)
        else:
            cur = keep + exchange(send, axis, bit)
        chunks //= 2
        bit += 1
    return cur.reshape(head + (width,) + tail)


def gather_bits(x, axis, dim, levels):
    me = lax.axis_index(axis)
    head, width, tail = x.shape[:dim], x.shape[dim], x.shape[dim + 1 :]
    cur = x.reshape(head + (1, width) + tail)
    chunks = 1
    for bit in range(levels):
        got = exchange(cur, axis, bit)
        low = (me >> bit) & 1 == 0
        first = jnp.where(low, cur, got)
        second = jnp.where(low, got, cur)
        cur = jnp.stack([first, second], dim).reshape(head + (chunks * 2, width) + tail)
        chunks *= 2
    return cur.reshape(head + (chunks * width,) + tail)


def sum_all(x, axis):
    size = lax.axis_size(axis)
    if not is_power_of_two(size):
        return lax.psum(x, axis)
    for bit in range(size.bit_length() - 1):
        x = x + exchange(x, axis, bit)
    return x


def merge_totals(first_set, second_set):
    larger = jnp.maximum(first_set[0], second_set[0])
    combined = first_set[1] * jnp.exp(first_set[0] - larger) + second_set[1] * jnp.exp(
        second_set[0] - larger
    )
    return jnp.stack([larger, combined, first_set[2] + second_set[2]])


def merge_all(stats, axis):
    size = lax.axis_size(axis)
    if is_power_of_two(size):
        for bit in range(size.bit_length() - 1):
            stats = merge_totals(stats, exchange(stats, axis, bit))
        return stats
    everything = lax.all_gather(stats, axis)
    return lax.fori_loop(1, size, lambda k, so_far: merge_totals(so_far, everything[k]), everything[0])


def body(
    dec_hidden,
    w_query,
    enc_states,
    w_out,
    norm_gain,
    w_vocab,
    enc_segment,
    dec_segment,
    seg_map,
    targets,
    loss_mask,
):
    dp_index = lax.axis_index("dp")
    fsdp_index = lax.axis_index("fsdp")
    dp_count = lax.axis_size("dp")
    fsdp_count = lax.axis_size("fsdp")
    dec_len, width = dec_hidden.shape
    enc_len = enc_states.shape[1]
    heads_here = w_query.shape[1] // HEAD_DIM
    segments = seg_map.shape[1]
    feature_count = width // fsdp_count
    vocab_here = w_vocab.shape[1]
    window = min(ENC_MOST, enc_len)
    split_fsdp = is_power_of_two(fsdp_count) and fsdp_count > 1
    levels = fsdp_count.bit_length() - 1

    rows = jnp.arange(dp_count)
    seg_ids = jnp.arange(segments)
    map_row = jnp.sum(jnp.where((rows == dp_index)[:, None], seg_map, 0), 0)
    sources = jnp.sum(
        jnp.where(dec_segment[:, None] == seg_ids[None, :], map_row[None, :], 0), 1
    )
    offsets = (seg_map[0] // segments) % dp_count
    hits = offsets[None, :] == rows[:, None]
    used = jnp.any(hits, 1)
    enc_rows = enc_segment.reshape(dp_count, enc_len)
    all_starts = jnp.sum(enc_rows[:, None, :] < seg_ids[None, :, None], 2)
    reader_hot = ((dp_index - rows) % dp_count)[:, None] == rows[None, :]
    reader_maps = jnp.sum(jnp.where(reader_hot[:, :, None], seg_map[None], 0), 1)
    send_seg = jnp.sum(jnp.where(hits, reader_maps, 0), 1) % segments
    my_starts = jnp.sum(jnp.where((rows == dp_index)[:, None], all_starts, 0), 0)
    send_start = jnp.clip(
        jnp.sum(jnp.where(send_seg[:, None] == seg_ids[None, :], my_starts[None, :], 0), 1),
        0,
        enc_len - window,
    )
    token_at = jnp.arange(enc_len)[None, None, :]
    send_pos = send_start[:, None] + jnp.arange(window)[None, :]
    pick = (token_at == send_pos[:, :, None]).astype(jnp.bfloat16)
    windows = jnp.einsum(
        "str,crf->sctf", pick, enc_states, preferred_element_type=jnp.float32
    ).astype(jnp.bfloat16)
    owner_hot = ((dp_index + rows) % dp_count)[:, None] == rows[None, :]
    owner_rows = jnp.sum(jnp.where(owner_hot[:, :, None], enc_rows[None], 0), 1)
    owner_starts = jnp.sum(jnp.where(owner_hot[:, :, None], all_starts[None], 0), 1)
    served = jnp.sum(jnp.where(hits, map_row[None, :], 0), 1)
    served_local = served % segments
    recv_start = jnp.clip(
        jnp.sum(jnp.where(served_local[:, None] == seg_ids[None, :], owner_starts, 0), 1),
        0,
        enc_len - window,
    )
    recv_pos = recv_start[:, None] + jnp.arange(window)[None, :]
    seg_at = jnp.sum(jnp.where(token_at == recv_pos[:, :, None], owner_rows[:, None, :], 0), 2)
    key_ids = jnp.where(used[:, None] & (seg_at == served_local[:, None]), served[:, None], -1)

    query_proj = jnp.dot(dec_hidden, w_query, preferred_element_type=jnp.float32).astype(
        jnp.bfloat16
    )
    queries = lax.optimization_barrier(query_proj).reshape(dec_len, heads_here, HEAD_DIM)
    run_sum = jnp.zeros((heads_here, dec_len), jnp.float32)
    run_acc = jnp.zeros((heads_here, dec_len, HEAD_DIM), jnp.float32)
    for shift in range(dp_count):
        block = windows[shift]
        if shift:
            block = lax.ppermute(
                block, "dp", [(i, (i - shift) % dp_count) for i in range(dp_count)]
            )
        keys_here = block[0].reshape(window, heads_here, HEAD_DIM)
        values_here = block[1].astype(jnp.float32).reshape(window, heads_here, HEAD_DIM)
        scores = jnp.einsum(
            "ihd,jhd->hij", queries, keys_here, preferred_element_type=jnp.float32
        )
        allowed = (sources[:, None] == key_ids[shift][None, :])[None]
        top = jnp.max(jnp.where(allowed, scores, jnp.float32(-1e30)), 2)
        weights = jnp.where(allowed, jnp.exp(scores - top[:, :, None]), 0.0)
        run_sum = run_sum + jnp.sum(weights, 2)
        run_acc = run_acc + jnp.einsum("hij,jhd->hid", weights, values_here)
    attended = (
        (run_acc / run_sum[:, :, None])
        .transpose(1, 0, 2)
        .reshape(dec_len, heads_here * HEAD_DIM)
        .astype(jnp.bfloat16)
    )

    feature_start = fsdp_index * feature_count
    gain_part = lax.dynamic_slice_in_dim(norm_gain, feature_start, feature_count, 0)
    hidden_part = lax.dynamic_slice_in_dim(dec_hidden, feature_start, feature_count, 1)
    projected = lax.optimization_barrier(
        jnp.dot(attended, w_out, preferred_element_type=jnp.float32)
    )
    if split_fsdp:
        projected = scatter_bits(projected, "fsdp", 1, levels, jnp.bfloat16)
    else:
        projected = lax.psum_scatter(projected, "fsdp", scatter_dimension=1, tiled=True)
    summed_part = projected + hidden_part.astype(jnp.float32)
    square_total = sum_all(jnp.sum(summed_part * summed_part, 1), "fsdp")
    inv_root = lax.rsqrt(square_total / width + 1e-06)
    unit_part = summed_part * inv_root[:, None]
    normed_part = (unit_part * gain_part).astype(jnp.bfloat16)
    if split_fsdp:
        half = width // 2
        top_side = (fsdp_index >> (levels - 1)) & 1
        near_rows = lax.dynamic_slice_in_dim(w_vocab, top_side * half, half, 0)
        far_rows = lax.dynamic_slice_in_dim(w_vocab, (1 - top_side) * half, half, 0)
        near_normed = gather_bits(normed_part, "fsdp", 1, levels - 1)
        far_normed = exchange(near_normed, "fsdp", levels - 1)
        logits = jnp.dot(near_normed, near_rows, preferred_element_type=jnp.float32) + jnp.dot(
            far_normed, far_rows, preferred_element_type=jnp.float32
        )
    else:
        normed_full = lax.all_gather(normed_part, "fsdp", axis=1, tiled=True)
        logits = jnp.dot(normed_full, w_vocab, preferred_element_type=jnp.float32)
    local_target = targets - fsdp_index * vocab_here
    picked = jnp.arange(vocab_here)[None, :] == local_target[:, None]
    local_top = jnp.max(logits, 1)
    local_total = jnp.sum(jnp.exp(logits - local_top[:, None]), 1)
    local_pick = jnp.sum(jnp.where(picked, logits, 0.0), 1)
    row_top, row_total, target_logit = merge_all(
        jnp.stack([local_top, local_total, local_pick]), "fsdp"
    )
    log_total = row_top + jnp.log(row_total)
    mask_float = loss_mask.astype(jnp.float32)
    grad_logits = (
        mask_float[:, None] * (jnp.exp(logits - log_total[:, None]) - picked.astype(jnp.float32))
    ).astype(jnp.bfloat16)
    contract = (((1,), (1,)), ((), ()))
    if split_fsdp:
        far_grad = lax.dot_general(
            far_rows, grad_logits, contract, preferred_element_type=jnp.float32
        )
        far_grad, near_logits = lax.optimization_barrier(
            (scatter_bits(far_grad, "fsdp", 0, levels - 1), grad_logits)
        )
        far_grad = exchange(far_grad.astype(jnp.bfloat16), "fsdp", levels - 1).astype(
            jnp.float32
        )
        near_grad = lax.dot_general(
            near_rows, near_logits, contract, preferred_element_type=jnp.float32
        )
        grad_normed = (scatter_bits(near_grad, "fsdp", 0, levels - 1) + far_grad).T
    else:
        grad_normed = lax.psum_scatter(
            lax.dot_general(w_vocab, grad_logits, contract, preferred_element_type=jnp.float32),
            "fsdp",
            scatter_dimension=0,
            tiled=True,
        ).T
    grad_unit = grad_normed * gain_part
    inner_total = sum_all(jnp.sum(grad_unit * unit_part, 1), "fsdp")
    grad_summed = inv_root[:, None] * (grad_unit - unit_part * (inner_total / width)[:, None])
    gain_local = jnp.sum(grad_normed * unit_part, 0)
    packed = jnp.concatenate(
        [jnp.stack([jnp.sum(mask_float), jnp.sum(mask_float * (log_total - target_logit))]), gain_local]
    )
    packed = sum_all(packed, "dp")
    token_count, loss_total, gain_total = packed[0], packed[1], packed[2:]
    return (
        loss_total / token_count,
        (grad_summed / token_count).astype(jnp.bfloat16),
        gain_total / token_count,
    )


def solution(mesh):
    in_specs = (
        P("dp", None),
        P(None, "fsdp"),
        P(None, "dp", "fsdp"),
        P("fsdp", None),
        P(),
        P(None, "fsdp"),
        P(),
        P("dp"),
        P(),
        P("dp"),
        P("dp"),
    )
    out_specs = (P(), P("dp", "fsdp"), P("fsdp"))
    return jax.shard_map(body, mesh=mesh, in_specs=in_specs, out_specs=out_specs, check_vma=False)
```

```python
import jax
import jax.numpy as jnp
from jax import lax
from jax.sharding import PartitionSpec as P

HEAD_DIM = 64
ENC_MOST = 80


def is_power_of_two(n):
    return n & (n - 1) == 0


def exchange(x, axis, bit):
    size = lax.axis_size(axis)
    return lax.ppermute(x, axis, [(i, i ^ (1 << bit)) for i in range(size)])


def scatter_bits(x, axis, dim, levels, last_wire=None):
    me = lax.axis_index(axis)
    chunks = 1 << levels
    head, width, tail = x.shape[:dim], x.shape[dim] // chunks, x.shape[dim + 1 :]
    cur = x
    bit = 0
    while chunks > 1:
        cur = cur.reshape(head + (chunks // 2, 2, width) + tail)
        low = (me >> bit) & 1 == 0
        first = lax.index_in_dim(cur, 0, dim + 1, keepdims=False)
        second = lax.index_in_dim(cur, 1, dim + 1, keepdims=False)
        keep = jnp.where(low, first, second)
        send = jnp.where(low, second, first)
        if last_wire is not None and chunks == 2:
            cur = keep + exchange(send.astype(last_wire), axis, bit).astype(keep.dtype)
        else:
            cur = keep + exchange(send, axis, bit)
        chunks //= 2
        bit += 1
    return cur.reshape(head + (width,) + tail)


def gather_bits(x, axis, dim, levels):
    me = lax.axis_index(axis)
    head, width, tail = x.shape[:dim], x.shape[dim], x.shape[dim + 1 :]
    cur = x.reshape(head + (1, width) + tail)
    chunks = 1
    for bit in range(levels):
        got = exchange(cur, axis, bit)
        low = (me >> bit) & 1 == 0
        first = jnp.where(low, cur, got)
        second = jnp.where(low, got, cur)
        cur = jnp.stack([first, second], dim).reshape(head + (chunks * 2, width) + tail)
        chunks *= 2
    return cur.reshape(head + (chunks * width,) + tail)


def sum_all(x, axis):
    size = lax.axis_size(axis)
    if not is_power_of_two(size):
        return lax.psum(x, axis)
    for bit in range(size.bit_length() - 1):
        x = x + exchange(x, axis, bit)
    return x


def merge_totals(first_set, second_set):
    larger = jnp.maximum(first_set[0], second_set[0])
    combined = first_set[1] * jnp.exp(first_set[0] - larger) + second_set[1] * jnp.exp(
        second_set[0] - larger
    )
    return jnp.stack([larger, combined, first_set[2] + second_set[2]])


def merge_all(stats, axis):
    size = lax.axis_size(axis)
    if is_power_of_two(size):
        for bit in range(size.bit_length() - 1):
            stats = merge_totals(stats, exchange(stats, axis, bit))
        return stats
    everything = lax.all_gather(stats, axis)
    return lax.fori_loop(1, size, lambda k, so_far: merge_totals(so_far, everything[k]), everything[0])


def body(
    dec_hidden,
    w_query,
    enc_states,
    w_out,
    norm_gain,
    w_vocab,
    enc_segment,
    dec_segment,
    seg_map,
    targets,
    loss_mask,
):
    dp_index = lax.axis_index("dp")
    fsdp_index = lax.axis_index("fsdp")
    dp_count = lax.axis_size("dp")
    fsdp_count = lax.axis_size("fsdp")
    dec_len, width = dec_hidden.shape
    enc_len = enc_states.shape[1]
    heads_here = w_query.shape[1] // HEAD_DIM
    segments = seg_map.shape[1]
    feature_count = width // fsdp_count
    vocab_here = w_vocab.shape[1]
    window = min(ENC_MOST, enc_len)
    split_fsdp = is_power_of_two(fsdp_count) and fsdp_count > 1
    levels = fsdp_count.bit_length() - 1

    rows = jnp.arange(dp_count)
    seg_ids = jnp.arange(segments)
    map_row = jnp.sum(jnp.where((rows == dp_index)[:, None], seg_map, 0), 0)
    sources = jnp.sum(
        jnp.where(dec_segment[:, None] == seg_ids[None, :], map_row[None, :], 0), 1
    )
    offsets = (seg_map[0] // segments) % dp_count
    hits = offsets[None, :] == rows[:, None]
    used = jnp.any(hits, 1)
    enc_rows = enc_segment.reshape(dp_count, enc_len)
    all_starts = jnp.sum(enc_rows[:, None, :] < seg_ids[None, :, None], 2)
    reader_hot = ((dp_index - rows) % dp_count)[:, None] == rows[None, :]
    reader_maps = jnp.sum(jnp.where(reader_hot[:, :, None], seg_map[None], 0), 1)
    send_seg = jnp.sum(jnp.where(hits, reader_maps, 0), 1) % segments
    my_starts = jnp.sum(jnp.where((rows == dp_index)[:, None], all_starts, 0), 0)
    send_start = jnp.clip(
        jnp.sum(jnp.where(send_seg[:, None] == seg_ids[None, :], my_starts[None, :], 0), 1),
        0,
        enc_len - window,
    )
    token_at = jnp.arange(enc_len)[None, None, :]
    send_pos = send_start[:, None] + jnp.arange(window)[None, :]
    pick = (token_at == send_pos[:, :, None]).astype(jnp.bfloat16)
    windows = jnp.einsum(
        "str,crf->sctf", pick, enc_states, preferred_element_type=jnp.float32
    ).astype(jnp.bfloat16)
    owner_hot = ((dp_index + rows) % dp_count)[:, None] == rows[None, :]
    owner_rows = jnp.sum(jnp.where(owner_hot[:, :, None], enc_rows[None], 0), 1)
    owner_starts = jnp.sum(jnp.where(owner_hot[:, :, None], all_starts[None], 0), 1)
    served = jnp.sum(jnp.where(hits, map_row[None, :], 0), 1)
    served_local = served % segments
    recv_start = jnp.clip(
        jnp.sum(jnp.where(served_local[:, None] == seg_ids[None, :], owner_starts, 0), 1),
        0,
        enc_len - window,
    )
    recv_pos = recv_start[:, None] + jnp.arange(window)[None, :]
    seg_at = jnp.sum(jnp.where(token_at == recv_pos[:, :, None], owner_rows[:, None, :], 0), 2)
    key_ids = jnp.where(used[:, None] & (seg_at == served_local[:, None]), served[:, None], -1)

    query_proj = jnp.dot(dec_hidden, w_query, preferred_element_type=jnp.float32).astype(
        jnp.bfloat16
    )
    queries = lax.optimization_barrier(query_proj).reshape(dec_len, heads_here, HEAD_DIM)
    run_sum = jnp.zeros((heads_here, dec_len), jnp.float32)
    run_acc = jnp.zeros((heads_here, dec_len, HEAD_DIM), jnp.float32)
    for shift in range(dp_count):
        block = windows[shift]
        if shift:
            block = lax.ppermute(
                block, "dp", [(i, (i - shift) % dp_count) for i in range(dp_count)]
            )
        keys_here = block[0].reshape(window, heads_here, HEAD_DIM)
        values_here = block[1].astype(jnp.float32).reshape(window, heads_here, HEAD_DIM)
        scores = jnp.einsum(
            "ihd,jhd->hij", queries, keys_here, preferred_element_type=jnp.float32
        )
        allowed = (sources[:, None] == key_ids[shift][None, :])[None]
        top = jnp.max(jnp.where(allowed, scores, jnp.float32(-1e30)), 2)
        weights = jnp.where(allowed, jnp.exp(scores - top[:, :, None]), 0.0)
        run_sum = run_sum + jnp.sum(weights, 2)
        run_acc = run_acc + jnp.einsum("hij,jhd->hid", weights, values_here)
    attended = (
        (run_acc / run_sum[:, :, None])
        .transpose(1, 0, 2)
        .reshape(dec_len, heads_here * HEAD_DIM)
        .astype(jnp.bfloat16)
    )

    feature_start = fsdp_index * feature_count
    gain_part = lax.dynamic_slice_in_dim(norm_gain, feature_start, feature_count, 0)
    hidden_part = lax.dynamic_slice_in_dim(dec_hidden, feature_start, feature_count, 1)
    if split_fsdp:
        projected = lax.dot_general(
            w_out, attended, (((0,), (1,)), ((), ())), preferred_element_type=jnp.float32
        )
        projected = scatter_bits(projected, "fsdp", 0, levels, jnp.bfloat16).T
    else:
        projected = jnp.dot(attended, w_out, preferred_element_type=jnp.float32)
        projected = lax.psum_scatter(projected, "fsdp", scatter_dimension=1, tiled=True)
    summed_part = projected + hidden_part.astype(jnp.float32)
    square_total = sum_all(jnp.sum(summed_part * summed_part, 1), "fsdp")
    inv_root = lax.rsqrt(square_total / width + 1e-06)
    unit_part = summed_part * inv_root[:, None]
    normed_part = (unit_part * gain_part).astype(jnp.bfloat16)
    if split_fsdp:
        half = width // 2
        top_side = (fsdp_index >> (levels - 1)) & 1
        near_rows = lax.dynamic_slice_in_dim(w_vocab, top_side * half, half, 0)
        far_rows = lax.dynamic_slice_in_dim(w_vocab, (1 - top_side) * half, half, 0)
        near_normed = gather_bits(normed_part, "fsdp", 1, levels - 1)
        far_normed = exchange(near_normed, "fsdp", levels - 1)
        logits = jnp.dot(near_normed, near_rows, preferred_element_type=jnp.float32) + jnp.dot(
            far_normed, far_rows, preferred_element_type=jnp.float32
        )
    else:
        normed_full = lax.all_gather(normed_part, "fsdp", axis=1, tiled=True)
        logits = jnp.dot(normed_full, w_vocab, preferred_element_type=jnp.float32)
    local_target = targets - fsdp_index * vocab_here
    picked = jnp.arange(vocab_here)[None, :] == local_target[:, None]
    local_top = jnp.max(logits, 1)
    local_total = jnp.sum(jnp.exp(logits - local_top[:, None]), 1)
    local_pick = jnp.sum(jnp.where(picked, logits, 0.0), 1)
    row_top, row_total, target_logit = merge_all(
        jnp.stack([local_top, local_total, local_pick]), "fsdp"
    )
    log_total = row_top + jnp.log(row_total)
    mask_float = loss_mask.astype(jnp.float32)
    grad_logits = (
        mask_float[:, None] * (jnp.exp(logits - log_total[:, None]) - picked.astype(jnp.float32))
    ).astype(jnp.bfloat16)
    contract = (((1,), (1,)), ((), ()))
    if split_fsdp:
        far_grad = lax.dot_general(
            far_rows, grad_logits, contract, preferred_element_type=jnp.float32
        )
        far_grad, near_logits = lax.optimization_barrier(
            (scatter_bits(far_grad, "fsdp", 0, levels - 1), grad_logits)
        )
        far_grad = exchange(far_grad.astype(jnp.bfloat16), "fsdp", levels - 1).astype(
            jnp.float32
        )
        near_grad = lax.dot_general(
            near_rows, near_logits, contract, preferred_element_type=jnp.float32
        )
        grad_normed = (scatter_bits(near_grad, "fsdp", 0, levels - 1) + far_grad).T
    else:
        grad_normed = lax.psum_scatter(
            lax.dot_general(w_vocab, grad_logits, contract, preferred_element_type=jnp.float32),
            "fsdp",
            scatter_dimension=0,
            tiled=True,
        ).T
    grad_unit = grad_normed * gain_part
    inner_total = sum_all(jnp.sum(grad_unit * unit_part, 1), "fsdp")
    grad_summed = inv_root[:, None] * (grad_unit - unit_part * (inner_total / width)[:, None])
    gain_local = jnp.sum(grad_normed * unit_part, 0)
    packed = jnp.concatenate(
        [jnp.stack([jnp.sum(mask_float), jnp.sum(mask_float * (log_total - target_logit))]), gain_local]
    )
    packed = sum_all(packed, "dp")
    token_count, loss_total, gain_total = packed[0], packed[1], packed[2:]
    return (
        loss_total / token_count,
        (grad_summed / token_count).astype(jnp.bfloat16),
        gain_total / token_count,
    )


def solution(mesh):
    in_specs = (
        P("dp", None),
        P(None, "fsdp"),
        P(None, "dp", "fsdp"),
        P("fsdp", None),
        P(),
        P(None, "fsdp"),
        P(),
        P("dp"),
        P(),
        P("dp"),
        P("dp"),
    )
    out_specs = (P(), P("dp", "fsdp"), P("fsdp"))
    return jax.shard_map(body, mesh=mesh, in_specs=in_specs, out_specs=out_specs, check_vma=False)
```

```python
import jax
import jax.numpy as jnp
from jax import lax
from jax.sharding import PartitionSpec as P

HEAD_DIM = 64
ENC_MOST = 80


def is_power_of_two(n):
    return n & (n - 1) == 0


def exchange(x, axis, bit):
    size = lax.axis_size(axis)
    return lax.ppermute(x, axis, [(i, i ^ (1 << bit)) for i in range(size)])


def scatter_bits(x, axis, dim, levels, last_wire=None):
    me = lax.axis_index(axis)
    chunks = 1 << levels
    head, width, tail = x.shape[:dim], x.shape[dim] // chunks, x.shape[dim + 1 :]
    cur = x
    bit = 0
    while chunks > 1:
        cur = cur.reshape(head + (chunks // 2, 2, width) + tail)
        side = (me >> bit) & 1
        keep = lax.dynamic_index_in_dim(cur, side, dim + 1, keepdims=False)
        send = lax.dynamic_index_in_dim(cur, 1 - side, dim + 1, keepdims=False)
        if last_wire is not None and chunks == 2:
            cur = keep + exchange(send.astype(last_wire), axis, bit).astype(keep.dtype)
        else:
            cur = keep + exchange(send, axis, bit)
        chunks //= 2
        bit += 1
    return cur.reshape(head + (width,) + tail)


def gather_bits(x, axis, dim, levels):
    me = lax.axis_index(axis)
    head, width, tail = x.shape[:dim], x.shape[dim], x.shape[dim + 1 :]
    cur = x.reshape(head + (1, width) + tail)
    chunks = 1
    for bit in range(levels):
        got = exchange(cur, axis, bit)
        low = (me >> bit) & 1 == 0
        first = jnp.where(low, cur, got)
        second = jnp.where(low, got, cur)
        cur = jnp.stack([first, second], dim).reshape(head + (chunks * 2, width) + tail)
        chunks *= 2
    return cur.reshape(head + (chunks * width,) + tail)


def sum_all(x, axis):
    size = lax.axis_size(axis)
    if not is_power_of_two(size):
        return lax.psum(x, axis)
    for bit in range(size.bit_length() - 1):
        x = x + exchange(x, axis, bit)
    return x


def merge_totals(first_set, second_set):
    larger = jnp.maximum(first_set[0], second_set[0])
    combined = first_set[1] * jnp.exp(first_set[0] - larger) + second_set[1] * jnp.exp(
        second_set[0] - larger
    )
    return jnp.stack([larger, combined, first_set[2] + second_set[2]])


def merge_all(stats, axis):
    size = lax.axis_size(axis)
    if is_power_of_two(size):
        for bit in range(size.bit_length() - 1):
            stats = merge_totals(stats, exchange(stats, axis, bit))
        return stats
    everything = lax.all_gather(stats, axis)
    return lax.fori_loop(1, size, lambda k, so_far: merge_totals(so_far, everything[k]), everything[0])


def body(
    dec_hidden,
    w_query,
    enc_states,
    w_out,
    norm_gain,
    w_vocab,
    enc_segment,
    dec_segment,
    seg_map,
    targets,
    loss_mask,
):
    dp_index = lax.axis_index("dp")
    fsdp_index = lax.axis_index("fsdp")
    dp_count = lax.axis_size("dp")
    fsdp_count = lax.axis_size("fsdp")
    dec_len, width = dec_hidden.shape
    enc_len = enc_states.shape[1]
    heads_here = w_query.shape[1] // HEAD_DIM
    segments = seg_map.shape[1]
    feature_count = width // fsdp_count
    vocab_here = w_vocab.shape[1]
    window = min(ENC_MOST, enc_len)
    split_fsdp = is_power_of_two(fsdp_count) and fsdp_count > 1
    levels = fsdp_count.bit_length() - 1

    rows = jnp.arange(dp_count)
    seg_ids = jnp.arange(segments)
    map_row = jnp.sum(jnp.where((rows == dp_index)[:, None], seg_map, 0), 0)
    sources = jnp.sum(
        jnp.where(dec_segment[:, None] == seg_ids[None, :], map_row[None, :], 0), 1
    )
    offsets = (seg_map[0] // segments) % dp_count
    hits = offsets[None, :] == rows[:, None]
    used = jnp.any(hits, 1)
    enc_rows = enc_segment.reshape(dp_count, enc_len)
    all_starts = jnp.sum(enc_rows[:, None, :] < seg_ids[None, :, None], 2)
    reader_hot = ((dp_index - rows) % dp_count)[:, None] == rows[None, :]
    reader_maps = jnp.sum(jnp.where(reader_hot[:, :, None], seg_map[None], 0), 1)
    send_seg = jnp.sum(jnp.where(hits, reader_maps, 0), 1) % segments
    my_starts = jnp.sum(jnp.where((rows == dp_index)[:, None], all_starts, 0), 0)
    send_start = jnp.clip(
        jnp.sum(jnp.where(send_seg[:, None] == seg_ids[None, :], my_starts[None, :], 0), 1),
        0,
        enc_len - window,
    )
    token_at = jnp.arange(enc_len)[None, None, :]
    send_pos = send_start[:, None] + jnp.arange(window)[None, :]
    pick = (token_at == send_pos[:, :, None]).astype(jnp.bfloat16)
    windows = jnp.einsum(
        "str,crf->sctf", pick, enc_states, preferred_element_type=jnp.float32
    ).astype(jnp.bfloat16)
    owner_hot = ((dp_index + rows) % dp_count)[:, None] == rows[None, :]
    owner_rows = jnp.sum(jnp.where(owner_hot[:, :, None], enc_rows[None], 0), 1)
    owner_starts = jnp.sum(jnp.where(owner_hot[:, :, None], all_starts[None], 0), 1)
    served = jnp.sum(jnp.where(hits, map_row[None, :], 0), 1)
    served_local = served % segments
    recv_start = jnp.clip(
        jnp.sum(jnp.where(served_local[:, None] == seg_ids[None, :], owner_starts, 0), 1),
        0,
        enc_len - window,
    )
    recv_pos = recv_start[:, None] + jnp.arange(window)[None, :]
    seg_at = jnp.sum(jnp.where(token_at == recv_pos[:, :, None], owner_rows[:, None, :], 0), 2)
    key_ids = jnp.where(used[:, None] & (seg_at == served_local[:, None]), served[:, None], -1)

    query_proj = jnp.dot(dec_hidden, w_query, preferred_element_type=jnp.float32).astype(
        jnp.bfloat16
    )
    queries = lax.optimization_barrier(query_proj).reshape(dec_len, heads_here, HEAD_DIM)
    run_sum = jnp.zeros((heads_here, dec_len), jnp.float32)
    run_acc = jnp.zeros((heads_here, dec_len, HEAD_DIM), jnp.float32)
    for shift in range(dp_count):
        block = windows[shift]
        if shift:
            pairs = [(i, (i - shift) % dp_count) for i in range(dp_count)]
            if shift in (dp_count // 2, dp_count - 1):
                block = lax.ppermute(block, "dp", pairs)
            else:
                block = lax.cond(
                    used[shift], lambda b: lax.ppermute(b, "dp", pairs), lambda b: b, block
                )
        keys_here = block[0].reshape(window, heads_here, HEAD_DIM)
        values_here = block[1].astype(jnp.float32).reshape(window, heads_here, HEAD_DIM)
        scores = jnp.einsum(
            "ihd,jhd->hij", queries, keys_here, preferred_element_type=jnp.float32
        )
        allowed = (sources[:, None] == key_ids[shift][None, :])[None]
        top = jnp.max(jnp.where(allowed, scores, jnp.float32(-1e30)), 2)
        weights = jnp.where(allowed, jnp.exp(scores - top[:, :, None]), 0.0)
        run_sum = run_sum + jnp.sum(weights, 2)
        run_acc = run_acc + jnp.einsum("hij,jhd->hid", weights, values_here)
    attended = (
        (run_acc / run_sum[:, :, None])
        .transpose(1, 0, 2)
        .reshape(dec_len, heads_here * HEAD_DIM)
        .astype(jnp.bfloat16)
    )

    feature_start = fsdp_index * feature_count
    gain_part = lax.dynamic_slice_in_dim(norm_gain, feature_start, feature_count, 0)
    hidden_part = lax.dynamic_slice_in_dim(dec_hidden, feature_start, feature_count, 1)
    projected = lax.optimization_barrier(
        jnp.dot(attended, w_out, preferred_element_type=jnp.float32)
    )
    if split_fsdp:
        projected = scatter_bits(projected, "fsdp", 1, levels, jnp.bfloat16)
    else:
        projected = lax.psum_scatter(projected, "fsdp", scatter_dimension=1, tiled=True)
    summed_part = projected + hidden_part.astype(jnp.float32)
    square_total = sum_all(jnp.sum(summed_part * summed_part, 1), "fsdp")
    inv_root = lax.rsqrt(square_total / width + 1e-06)
    unit_part = summed_part * inv_root[:, None]
    normed_part = (unit_part * gain_part).astype(jnp.bfloat16)
    if split_fsdp:
        half = width // 2
        top_side = (fsdp_index >> (levels - 1)) & 1
        near_rows = lax.dynamic_slice_in_dim(w_vocab, top_side * half, half, 0)
        far_rows = lax.dynamic_slice_in_dim(w_vocab, (1 - top_side) * half, half, 0)
        near_normed = gather_bits(normed_part, "fsdp", 1, levels - 1)
        far_normed = exchange(near_normed, "fsdp", levels - 1)
        logits = jnp.dot(near_normed, near_rows, preferred_element_type=jnp.float32) + jnp.dot(
            far_normed, far_rows, preferred_element_type=jnp.float32
        )
    else:
        normed_full = lax.all_gather(normed_part, "fsdp", axis=1, tiled=True)
        logits = jnp.dot(normed_full, w_vocab, preferred_element_type=jnp.float32)
    local_target = targets - fsdp_index * vocab_here
    picked = jnp.arange(vocab_here)[None, :] == local_target[:, None]
    local_top = jnp.max(logits, 1)
    local_total = jnp.sum(jnp.exp(logits - local_top[:, None]), 1)
    local_pick = jnp.sum(jnp.where(picked, logits, 0.0), 1)
    row_top, row_total, target_logit = merge_all(
        jnp.stack([local_top, local_total, local_pick]), "fsdp"
    )
    log_total = row_top + jnp.log(row_total)
    mask_float = loss_mask.astype(jnp.float32)
    grad_logits = (
        mask_float[:, None] * (jnp.exp(logits - log_total[:, None]) - picked.astype(jnp.float32))
    ).astype(jnp.bfloat16)
    contract = (((1,), (1,)), ((), ()))
    if split_fsdp:
        far_grad = lax.dot_general(
            far_rows, grad_logits, contract, preferred_element_type=jnp.float32
        )
        far_grad, near_logits = lax.optimization_barrier(
            (scatter_bits(far_grad, "fsdp", 0, levels - 1), grad_logits)
        )
        far_grad = exchange(far_grad.astype(jnp.bfloat16), "fsdp", levels - 1).astype(
            jnp.float32
        )
        near_grad = lax.dot_general(
            near_rows, near_logits, contract, preferred_element_type=jnp.float32
        )
        grad_normed = (scatter_bits(near_grad, "fsdp", 0, levels - 1) + far_grad).T
    else:
        grad_normed = lax.psum_scatter(
            lax.dot_general(w_vocab, grad_logits, contract, preferred_element_type=jnp.float32),
            "fsdp",
            scatter_dimension=0,
            tiled=True,
        ).T
    grad_unit = grad_normed * gain_part
    inner_total = sum_all(jnp.sum(grad_unit * unit_part, 1), "fsdp")
    grad_summed = inv_root[:, None] * (grad_unit - unit_part * (inner_total / width)[:, None])
    gain_local = jnp.sum(grad_normed * unit_part, 0)
    packed = jnp.concatenate(
        [jnp.stack([jnp.sum(mask_float), jnp.sum(mask_float * (log_total - target_logit))]), gain_local]
    )
    packed = sum_all(packed, "dp")
    token_count, loss_total, gain_total = packed[0], packed[1], packed[2:]
    return (
        loss_total / token_count,
        (grad_summed / token_count).astype(jnp.bfloat16),
        gain_total / token_count,
    )


def solution(mesh):
    in_specs = (
        P("dp", None),
        P(None, "fsdp"),
        P(None, "dp", "fsdp"),
        P("fsdp", None),
        P(),
        P(None, "fsdp"),
        P(),
        P("dp"),
        P(),
        P("dp"),
        P("dp"),
    )
    out_specs = (P(), P("dp", "fsdp"), P("fsdp"))
    return jax.shard_map(body, mesh=mesh, in_specs=in_specs, out_specs=out_specs, check_vma=False)
```

```python
import jax
import jax.numpy as jnp
from jax import lax
from jax.sharding import PartitionSpec as P

HEAD_DIM = 64
ENC_MOST = 80


def is_power_of_two(n):
    return n & (n - 1) == 0


def exchange(x, axis, bit):
    size = lax.axis_size(axis)
    return lax.ppermute(x, axis, [(i, i ^ (1 << bit)) for i in range(size)])


def scatter_bits(x, axis, dim, levels, last_wire=None):
    me = lax.axis_index(axis)
    chunks = 1 << levels
    head, width, tail = x.shape[:dim], x.shape[dim] // chunks, x.shape[dim + 1 :]
    cur = x
    bit = 0
    while chunks > 1:
        cur = cur.reshape(head + (chunks // 2, 2, width) + tail)
        side = (me >> bit) & 1
        keep = lax.dynamic_index_in_dim(cur, side, dim + 1, keepdims=False)
        send = lax.dynamic_index_in_dim(cur, 1 - side, dim + 1, keepdims=False)
        if last_wire is not None and chunks == 2:
            cur = keep + exchange(send.astype(last_wire), axis, bit).astype(keep.dtype)
        else:
            cur = keep + exchange(send, axis, bit)
        chunks //= 2
        bit += 1
    return cur.reshape(head + (width,) + tail)


def gather_bits(x, axis, dim, levels):
    me = lax.axis_index(axis)
    head, width, tail = x.shape[:dim], x.shape[dim], x.shape[dim + 1 :]
    cur = x.reshape(head + (1, width) + tail)
    chunks = 1
    for bit in range(levels):
        got = exchange(cur, axis, bit)
        low = (me >> bit) & 1 == 0
        first = jnp.where(low, cur, got)
        second = jnp.where(low, got, cur)
        cur = jnp.stack([first, second], dim).reshape(head + (chunks * 2, width) + tail)
        chunks *= 2
    return cur.reshape(head + (chunks * width,) + tail)


def by_source(x, axis):
    size = lax.axis_size(axis)
    me = lax.axis_index(axis)
    pieces = [x]
    for shift in range(1, size):
        pieces.append(lax.ppermute(x, axis, [(i, (i - shift) % size) for i in range(size)]))
    stacked = jnp.stack(pieces)
    order = (jnp.arange(size)[:, None] - me) % size == jnp.arange(size)[None, :]
    hot = order.reshape((size, size) + (1,) * x.ndim)
    return jnp.sum(jnp.where(hot, stacked[None], 0), 1)


def sum_all(x, axis):
    size = lax.axis_size(axis)
    if size > 16:
        return lax.psum(x, axis)
    return jnp.sum(by_source(x, axis), 0)


def merge_totals(first_set, second_set):
    larger = jnp.maximum(first_set[0], second_set[0])
    combined = first_set[1] * jnp.exp(first_set[0] - larger) + second_set[1] * jnp.exp(
        second_set[0] - larger
    )
    return jnp.stack([larger, combined, first_set[2] + second_set[2]])


def merge_all(stats, axis):
    size = lax.axis_size(axis)
    if size <= 16:
        everything = by_source(stats, axis)
        larger = jnp.max(everything[:, 0], 0)
        combined = jnp.sum(everything[:, 1] * jnp.exp(everything[:, 0] - larger[None]), 0)
        return jnp.stack([larger, combined, jnp.sum(everything[:, 2], 0)])
    everything = lax.all_gather(stats, axis)
    return lax.fori_loop(1, size, lambda k, so_far: merge_totals(so_far, everything[k]), everything[0])


def body(
    dec_hidden,
    w_query,
    enc_states,
    w_out,
    norm_gain,
    w_vocab,
    enc_segment,
    dec_segment,
    seg_map,
    targets,
    loss_mask,
):
    dp_index = lax.axis_index("dp")
    fsdp_index = lax.axis_index("fsdp")
    dp_count = lax.axis_size("dp")
    fsdp_count = lax.axis_size("fsdp")
    dec_len, width = dec_hidden.shape
    enc_len = enc_states.shape[1]
    heads_here = w_query.shape[1] // HEAD_DIM
    segments = seg_map.shape[1]
    feature_count = width // fsdp_count
    vocab_here = w_vocab.shape[1]
    window = min(ENC_MOST, enc_len)
    split_fsdp = is_power_of_two(fsdp_count) and fsdp_count > 1
    levels = fsdp_count.bit_length() - 1

    rows = jnp.arange(dp_count)
    seg_ids = jnp.arange(segments)
    map_row = jnp.sum(jnp.where((rows == dp_index)[:, None], seg_map, 0), 0)
    sources = jnp.sum(
        jnp.where(dec_segment[:, None] == seg_ids[None, :], map_row[None, :], 0), 1
    )
    offsets = (seg_map[0] // segments) % dp_count
    hits = offsets[None, :] == rows[:, None]
    used = jnp.any(hits, 1)
    enc_rows = enc_segment.reshape(dp_count, enc_len)
    all_starts = jnp.sum(enc_rows[:, None, :] < seg_ids[None, :, None], 2)
    reader_hot = ((dp_index - rows) % dp_count)[:, None] == rows[None, :]
    reader_maps = jnp.sum(jnp.where(reader_hot[:, :, None], seg_map[None], 0), 1)
    send_seg = jnp.sum(jnp.where(hits, reader_maps, 0), 1) % segments
    my_starts = jnp.sum(jnp.where((rows == dp_index)[:, None], all_starts, 0), 0)
    send_start = jnp.clip(
        jnp.sum(jnp.where(send_seg[:, None] == seg_ids[None, :], my_starts[None, :], 0), 1),
        0,
        enc_len - window,
    )
    token_at = jnp.arange(enc_len)[None, None, :]
    send_pos = send_start[:, None] + jnp.arange(window)[None, :]
    pick = (token_at == send_pos[:, :, None]).astype(jnp.bfloat16)
    windows = jnp.einsum(
        "str,crf->sctf", pick, enc_states, preferred_element_type=jnp.float32
    ).astype(jnp.bfloat16)
    owner_hot = ((dp_index + rows) % dp_count)[:, None] == rows[None, :]
    owner_rows = jnp.sum(jnp.where(owner_hot[:, :, None], enc_rows[None], 0), 1)
    owner_starts = jnp.sum(jnp.where(owner_hot[:, :, None], all_starts[None], 0), 1)
    served = jnp.sum(jnp.where(hits, map_row[None, :], 0), 1)
    served_local = served % segments
    recv_start = jnp.clip(
        jnp.sum(jnp.where(served_local[:, None] == seg_ids[None, :], owner_starts, 0), 1),
        0,
        enc_len - window,
    )
    recv_pos = recv_start[:, None] + jnp.arange(window)[None, :]
    seg_at = jnp.sum(jnp.where(token_at == recv_pos[:, :, None], owner_rows[:, None, :], 0), 2)
    key_ids = jnp.where(used[:, None] & (seg_at == served_local[:, None]), served[:, None], -1)

    query_proj = jnp.dot(dec_hidden, w_query, preferred_element_type=jnp.float32).astype(
        jnp.bfloat16
    )
    queries = lax.optimization_barrier(query_proj).reshape(dec_len, heads_here, HEAD_DIM)
    run_sum = jnp.zeros((heads_here, dec_len), jnp.float32)
    run_acc = jnp.zeros((heads_here, dec_len, HEAD_DIM), jnp.float32)
    for shift in range(dp_count):
        block = windows[shift]
        if shift:
            block = lax.ppermute(
                block, "dp", [(i, (i - shift) % dp_count) for i in range(dp_count)]
            )
        keys_here = block[0].reshape(window, heads_here, HEAD_DIM)
        values_here = block[1].astype(jnp.float32).reshape(window, heads_here, HEAD_DIM)
        scores = jnp.einsum(
            "ihd,jhd->hij", queries, keys_here, preferred_element_type=jnp.float32
        )
        allowed = (sources[:, None] == key_ids[shift][None, :])[None]
        top = jnp.max(jnp.where(allowed, scores, jnp.float32(-1e30)), 2)
        weights = jnp.where(allowed, jnp.exp(scores - top[:, :, None]), 0.0)
        run_sum = run_sum + jnp.sum(weights, 2)
        run_acc = run_acc + jnp.einsum("hij,jhd->hid", weights, values_here)
    attended = (
        (run_acc / run_sum[:, :, None])
        .transpose(1, 0, 2)
        .reshape(dec_len, heads_here * HEAD_DIM)
        .astype(jnp.bfloat16)
    )

    feature_start = fsdp_index * feature_count
    gain_part = lax.dynamic_slice_in_dim(norm_gain, feature_start, feature_count, 0)
    hidden_part = lax.dynamic_slice_in_dim(dec_hidden, feature_start, feature_count, 1)
    projected = lax.optimization_barrier(
        jnp.dot(attended, w_out, preferred_element_type=jnp.float32)
    )
    if split_fsdp:
        projected = scatter_bits(projected, "fsdp", 1, levels, jnp.bfloat16)
    else:
        projected = lax.psum_scatter(projected, "fsdp", scatter_dimension=1, tiled=True)
    summed_part = projected + hidden_part.astype(jnp.float32)
    square_total = sum_all(jnp.sum(summed_part * summed_part, 1), "fsdp")
    inv_root = lax.rsqrt(square_total / width + 1e-06)
    unit_part = summed_part * inv_root[:, None]
    normed_part = (unit_part * gain_part).astype(jnp.bfloat16)
    if split_fsdp:
        half = width // 2
        top_side = (fsdp_index >> (levels - 1)) & 1
        near_rows = lax.dynamic_slice_in_dim(w_vocab, top_side * half, half, 0)
        far_rows = lax.dynamic_slice_in_dim(w_vocab, (1 - top_side) * half, half, 0)
        near_normed = gather_bits(normed_part, "fsdp", 1, levels - 1)
        far_normed = exchange(near_normed, "fsdp", levels - 1)
        logits = jnp.dot(near_normed, near_rows, preferred_element_type=jnp.float32) + jnp.dot(
            far_normed, far_rows, preferred_element_type=jnp.float32
        )
    else:
        normed_full = lax.all_gather(normed_part, "fsdp", axis=1, tiled=True)
        logits = jnp.dot(normed_full, w_vocab, preferred_element_type=jnp.float32)
    local_target = targets - fsdp_index * vocab_here
    picked = jnp.arange(vocab_here)[None, :] == local_target[:, None]
    local_top = jnp.max(logits, 1)
    local_total = jnp.sum(jnp.exp(logits - local_top[:, None]), 1)
    local_pick = jnp.sum(jnp.where(picked, logits, 0.0), 1)
    row_top, row_total, target_logit = merge_all(
        jnp.stack([local_top, local_total, local_pick]), "fsdp"
    )
    log_total = row_top + jnp.log(row_total)
    mask_float = loss_mask.astype(jnp.float32)
    grad_logits = (
        mask_float[:, None] * (jnp.exp(logits - log_total[:, None]) - picked.astype(jnp.float32))
    ).astype(jnp.bfloat16)
    contract = (((1,), (1,)), ((), ()))
    if split_fsdp:
        far_grad = lax.dot_general(
            far_rows, grad_logits, contract, preferred_element_type=jnp.float32
        )
        far_grad, near_logits = lax.optimization_barrier(
            (scatter_bits(far_grad, "fsdp", 0, levels - 1), grad_logits)
        )
        far_grad = exchange(far_grad.astype(jnp.bfloat16), "fsdp", levels - 1).astype(
            jnp.float32
        )
        near_grad = lax.dot_general(
            near_rows, near_logits, contract, preferred_element_type=jnp.float32
        )
        grad_normed = (scatter_bits(near_grad, "fsdp", 0, levels - 1) + far_grad).T
    else:
        grad_normed = lax.psum_scatter(
            lax.dot_general(w_vocab, grad_logits, contract, preferred_element_type=jnp.float32),
            "fsdp",
            scatter_dimension=0,
            tiled=True,
        ).T
    grad_unit = grad_normed * gain_part
    inner_total = sum_all(jnp.sum(grad_unit * unit_part, 1), "fsdp")
    grad_summed = inv_root[:, None] * (grad_unit - unit_part * (inner_total / width)[:, None])
    gain_local = jnp.sum(grad_normed * unit_part, 0)
    packed = jnp.concatenate(
        [jnp.stack([jnp.sum(mask_float), jnp.sum(mask_float * (log_total - target_logit))]), gain_local]
    )
    packed = sum_all(packed, "dp")
    token_count, loss_total, gain_total = packed[0], packed[1], packed[2:]
    return (
        loss_total / token_count,
        (grad_summed / token_count).astype(jnp.bfloat16),
        gain_total / token_count,
    )


def solution(mesh):
    in_specs = (
        P("dp", None),
        P(None, "fsdp"),
        P(None, "dp", "fsdp"),
        P("fsdp", None),
        P(),
        P(None, "fsdp"),
        P(),
        P("dp"),
        P(),
        P("dp"),
        P("dp"),
    )
    out_specs = (P(), P("dp", "fsdp"), P("fsdp"))
    return jax.shard_map(body, mesh=mesh, in_specs=in_specs, out_specs=out_specs, check_vma=False)
```

```python
import jax
import jax.numpy as jnp
from jax import lax
from jax.sharding import PartitionSpec as P

HEAD_DIM = 64
ENC_MOST = 80


def is_power_of_two(n):
    return n & (n - 1) == 0


def exchange(x, axis, bit):
    size = lax.axis_size(axis)
    return lax.ppermute(x, axis, [(i, i ^ (1 << bit)) for i in range(size)])


def scatter_bits(x, axis, dim, levels, last_wire=None):
    me = lax.axis_index(axis)
    chunks = 1 << levels
    head, width, tail = x.shape[:dim], x.shape[dim] // chunks, x.shape[dim + 1 :]
    cur = x
    bit = 0
    while chunks > 1:
        cur = cur.reshape(head + (chunks // 2, 2, width) + tail)
        side = (me >> bit) & 1
        keep = lax.dynamic_index_in_dim(cur, side, dim + 1, keepdims=False)
        send = lax.dynamic_index_in_dim(cur, 1 - side, dim + 1, keepdims=False)
        if last_wire is not None and chunks == 2:
            cur = keep + exchange(send.astype(last_wire), axis, bit).astype(keep.dtype)
        else:
            cur = keep + exchange(send, axis, bit)
        chunks //= 2
        bit += 1
    return cur.reshape(head + (width,) + tail)


def gather_bits(x, axis, dim, levels):
    me = lax.axis_index(axis)
    head, width, tail = x.shape[:dim], x.shape[dim], x.shape[dim + 1 :]
    cur = x.reshape(head + (1, width) + tail)
    chunks = 1
    for bit in range(levels):
        got = exchange(cur, axis, bit)
        low = (me >> bit) & 1 == 0
        first = jnp.where(low, cur, got)
        second = jnp.where(low, got, cur)
        cur = jnp.stack([first, second], dim).reshape(head + (chunks * 2, width) + tail)
        chunks *= 2
    return cur.reshape(head + (chunks * width,) + tail)


def sum_all(x, axis):
    size = lax.axis_size(axis)
    if not is_power_of_two(size):
        return lax.psum(x, axis)
    for bit in range(size.bit_length() - 1):
        x = x + exchange(x, axis, bit)
    return x


def merge_totals(first_set, second_set):
    larger = jnp.maximum(first_set[0], second_set[0])
    combined = first_set[1] * jnp.exp(first_set[0] - larger) + second_set[1] * jnp.exp(
        second_set[0] - larger
    )
    return jnp.stack([larger, combined, first_set[2] + second_set[2]])


def merge_all(stats, axis):
    size = lax.axis_size(axis)
    if is_power_of_two(size):
        for bit in range(size.bit_length() - 1):
            stats = merge_totals(stats, exchange(stats, axis, bit))
        return stats
    everything = lax.all_gather(stats, axis)
    return lax.fori_loop(1, size, lambda k, so_far: merge_totals(so_far, everything[k]), everything[0])


def body(
    dec_hidden,
    w_query,
    enc_states,
    w_out,
    norm_gain,
    w_vocab,
    enc_segment,
    dec_segment,
    seg_map,
    targets,
    loss_mask,
):
    dp_index = lax.axis_index("dp")
    fsdp_index = lax.axis_index("fsdp")
    dp_count = lax.axis_size("dp")
    fsdp_count = lax.axis_size("fsdp")
    dec_len, width = dec_hidden.shape
    enc_len = enc_states.shape[1]
    heads_here = w_query.shape[1] // HEAD_DIM
    segments = seg_map.shape[1]
    feature_count = width // fsdp_count
    vocab_here = w_vocab.shape[1]
    window = min(ENC_MOST, enc_len)
    split_fsdp = is_power_of_two(fsdp_count) and fsdp_count > 1
    levels = fsdp_count.bit_length() - 1

    rows = jnp.arange(dp_count)
    seg_ids = jnp.arange(segments)
    map_row = jnp.sum(jnp.where((rows == dp_index)[:, None], seg_map, 0), 0)
    sources = jnp.sum(
        jnp.where(dec_segment[:, None] == seg_ids[None, :], map_row[None, :], 0), 1
    )
    offsets = (seg_map[0] // segments) % dp_count
    hits = offsets[None, :] == rows[:, None]
    used = jnp.any(hits, 1)
    enc_rows = enc_segment.reshape(dp_count, enc_len)
    all_starts = jnp.sum(enc_rows[:, None, :] < seg_ids[None, :, None], 2)
    reader_hot = ((dp_index - rows) % dp_count)[:, None] == rows[None, :]
    reader_maps = jnp.sum(jnp.where(reader_hot[:, :, None], seg_map[None], 0), 1)
    send_seg = jnp.sum(jnp.where(hits, reader_maps, 0), 1) % segments
    my_starts = jnp.sum(jnp.where((rows == dp_index)[:, None], all_starts, 0), 0)
    send_start = jnp.clip(
        jnp.sum(jnp.where(send_seg[:, None] == seg_ids[None, :], my_starts[None, :], 0), 1),
        0,
        enc_len - window,
    )
    token_at = jnp.arange(enc_len)[None, None, :]
    send_pos = send_start[:, None] + jnp.arange(window)[None, :]
    pick = (token_at == send_pos[:, :, None]).astype(jnp.bfloat16)
    windows = jnp.einsum(
        "str,crf->sctf", pick, enc_states, preferred_element_type=jnp.float32
    ).astype(jnp.bfloat16)
    owner_hot = ((dp_index + rows) % dp_count)[:, None] == rows[None, :]
    owner_rows = jnp.sum(jnp.where(owner_hot[:, :, None], enc_rows[None], 0), 1)
    owner_starts = jnp.sum(jnp.where(owner_hot[:, :, None], all_starts[None], 0), 1)
    served = jnp.sum(jnp.where(hits, map_row[None, :], 0), 1)
    served_local = served % segments
    recv_start = jnp.clip(
        jnp.sum(jnp.where(served_local[:, None] == seg_ids[None, :], owner_starts, 0), 1),
        0,
        enc_len - window,
    )
    recv_pos = recv_start[:, None] + jnp.arange(window)[None, :]
    seg_at = jnp.sum(jnp.where(token_at == recv_pos[:, :, None], owner_rows[:, None, :], 0), 2)
    key_ids = jnp.where(used[:, None] & (seg_at == served_local[:, None]), served[:, None], -1)

    query_proj = jnp.dot(dec_hidden, w_query, preferred_element_type=jnp.float32).astype(
        jnp.bfloat16
    )
    queries = lax.optimization_barrier(query_proj).reshape(dec_len, heads_here, HEAD_DIM)
    run_sum = jnp.zeros((heads_here, dec_len), jnp.float32)
    run_acc = jnp.zeros((heads_here, dec_len, HEAD_DIM), jnp.float32)
    for shift in range(dp_count):
        block = windows[shift]
        if shift:
            block = lax.ppermute(
                block, "dp", [(i, (i - shift) % dp_count) for i in range(dp_count)]
            )
        keys_here = block[0].reshape(window, heads_here, HEAD_DIM)
        values_here = block[1].astype(jnp.float32).reshape(window, heads_here, HEAD_DIM)
        scores = jnp.einsum(
            "ihd,jhd->hij", queries, keys_here, preferred_element_type=jnp.float32
        )
        allowed = (sources[:, None] == key_ids[shift][None, :])[None]
        top = jnp.max(jnp.where(allowed, scores, jnp.float32(-1e30)), 2)
        weights = jnp.where(allowed, jnp.exp(scores - top[:, :, None]), 0.0)
        run_sum = run_sum + jnp.sum(weights, 2)
        run_acc = run_acc + jnp.einsum("hij,jhd->hid", weights, values_here)
    attended = (
        (run_acc / run_sum[:, :, None])
        .transpose(1, 0, 2)
        .reshape(dec_len, heads_here * HEAD_DIM)
        .astype(jnp.bfloat16)
    )

    feature_start = fsdp_index * feature_count
    gain_part = lax.dynamic_slice_in_dim(norm_gain, feature_start, feature_count, 0)
    hidden_part = lax.dynamic_slice_in_dim(dec_hidden, feature_start, feature_count, 1)
    projected = jnp.dot(attended, w_out, preferred_element_type=jnp.float32)
    if split_fsdp:
        projected = scatter_bits(projected, "fsdp", 1, levels, jnp.bfloat16)
    else:
        projected = lax.psum_scatter(projected, "fsdp", scatter_dimension=1, tiled=True)
    summed_part = projected + hidden_part.astype(jnp.float32)
    square_total = sum_all(jnp.sum(summed_part * summed_part, 1), "fsdp")
    inv_root = lax.rsqrt(square_total / width + 1e-06)
    unit_part = summed_part * inv_root[:, None]
    normed_part = (unit_part * gain_part).astype(jnp.bfloat16)
    if split_fsdp:
        half = width // 2
        top_side = (fsdp_index >> (levels - 1)) & 1
        near_rows = lax.dynamic_slice_in_dim(w_vocab, top_side * half, half, 0)
        far_rows = lax.dynamic_slice_in_dim(w_vocab, (1 - top_side) * half, half, 0)
        near_normed = gather_bits(normed_part, "fsdp", 1, levels - 1)
        far_normed = exchange(near_normed, "fsdp", levels - 1)
        logits = jnp.dot(near_normed, near_rows, preferred_element_type=jnp.float32) + jnp.dot(
            far_normed, far_rows, preferred_element_type=jnp.float32
        )
    else:
        normed_full = lax.all_gather(normed_part, "fsdp", axis=1, tiled=True)
        logits = jnp.dot(normed_full, w_vocab, preferred_element_type=jnp.float32)
    local_target = targets - fsdp_index * vocab_here
    picked = jnp.arange(vocab_here)[None, :] == local_target[:, None]
    local_top = jnp.max(logits, 1)
    local_total = jnp.sum(jnp.exp(logits - local_top[:, None]), 1)
    local_pick = jnp.sum(jnp.where(picked, logits, 0.0), 1)
    row_top, row_total, target_logit = merge_all(
        jnp.stack([local_top, local_total, local_pick]), "fsdp"
    )
    log_total = row_top + jnp.log(row_total)
    mask_float = loss_mask.astype(jnp.float32)
    grad_logits = (
        mask_float[:, None] * (jnp.exp(logits - log_total[:, None]) - picked.astype(jnp.float32))
    ).astype(jnp.bfloat16)
    contract = (((1,), (1,)), ((), ()))
    if split_fsdp:
        far_grad = lax.dot_general(
            far_rows, grad_logits, contract, preferred_element_type=jnp.float32
        )
        far_grad, near_logits = lax.optimization_barrier(
            (scatter_bits(far_grad, "fsdp", 0, levels - 1), grad_logits)
        )
        far_grad = exchange(far_grad.astype(jnp.bfloat16), "fsdp", levels - 1).astype(
            jnp.float32
        )
        near_grad = lax.dot_general(
            near_rows, near_logits, contract, preferred_element_type=jnp.float32
        )
        grad_normed = (scatter_bits(near_grad, "fsdp", 0, levels - 1) + far_grad).T
    else:
        grad_normed = lax.psum_scatter(
            lax.dot_general(w_vocab, grad_logits, contract, preferred_element_type=jnp.float32),
            "fsdp",
            scatter_dimension=0,
            tiled=True,
        ).T
    grad_unit = grad_normed * gain_part
    inner_total = sum_all(jnp.sum(grad_unit * unit_part, 1), "fsdp")
    grad_summed = inv_root[:, None] * (grad_unit - unit_part * (inner_total / width)[:, None])
    gain_local = jnp.sum(grad_normed * unit_part, 0)
    packed = jnp.concatenate(
        [jnp.stack([jnp.sum(mask_float), jnp.sum(mask_float * (log_total - target_logit))]), gain_local]
    )
    packed = sum_all(packed, "dp")
    token_count, loss_total, gain_total = packed[0], packed[1], packed[2:]
    return (
        loss_total / token_count,
        (grad_summed / token_count).astype(jnp.bfloat16),
        gain_total / token_count,
    )


def solution(mesh):
    in_specs = (
        P("dp", None),
        P(None, "fsdp"),
        P(None, "dp", "fsdp"),
        P("fsdp", None),
        P(),
        P(None, "fsdp"),
        P(),
        P("dp"),
        P(),
        P("dp"),
        P("dp"),
    )
    out_specs = (P(), P("dp", "fsdp"), P("fsdp"))
    return jax.shard_map(body, mesh=mesh, in_specs=in_specs, out_specs=out_specs, check_vma=False)
```

```python
import jax
import jax.numpy as jnp
from jax import lax
from jax.sharding import PartitionSpec as P

HEAD_DIM = 64
ENC_MOST = 80


def is_power_of_two(n):
    return n & (n - 1) == 0


def exchange(x, axis, bit):
    size = lax.axis_size(axis)
    return lax.ppermute(x, axis, [(i, i ^ (1 << bit)) for i in range(size)])


def scatter_bits(x, axis, dim, levels, last_wire=None):
    me = lax.axis_index(axis)
    chunks = 1 << levels
    head, width, tail = x.shape[:dim], x.shape[dim] // chunks, x.shape[dim + 1 :]
    cur = x
    bit = 0
    while chunks > 1:
        cur = cur.reshape(head + (chunks // 2, 2, width) + tail)
        side = (me >> bit) & 1
        keep = lax.dynamic_index_in_dim(cur, side, dim + 1, keepdims=False)
        send = lax.dynamic_index_in_dim(cur, 1 - side, dim + 1, keepdims=False)
        if last_wire is not None and chunks == 2:
            cur = keep + exchange(send.astype(last_wire), axis, bit).astype(keep.dtype)
        else:
            cur = keep + exchange(send, axis, bit)
        chunks //= 2
        bit += 1
    return cur.reshape(head + (width,) + tail)


def gather_bits(x, axis, dim, levels):
    me = lax.axis_index(axis)
    head, width, tail = x.shape[:dim], x.shape[dim], x.shape[dim + 1 :]
    cur = x.reshape(head + (1, width) + tail)
    chunks = 1
    for bit in range(levels):
        got = exchange(cur, axis, bit)
        low = (me >> bit) & 1 == 0
        first = jnp.where(low, cur, got)
        second = jnp.where(low, got, cur)
        cur = jnp.stack([first, second], dim).reshape(head + (chunks * 2, width) + tail)
        chunks *= 2
    return cur.reshape(head + (chunks * width,) + tail)


def sum_all(x, axis):
    size = lax.axis_size(axis)
    if not is_power_of_two(size):
        return lax.psum(x, axis)
    for bit in range(size.bit_length() - 1):
        x = x + exchange(x, axis, bit)
    return x


def merge_totals(first_set, second_set):
    larger = jnp.maximum(first_set[0], second_set[0])
    combined = first_set[1] * jnp.exp(first_set[0] - larger) + second_set[1] * jnp.exp(
        second_set[0] - larger
    )
    return jnp.stack([larger, combined, first_set[2] + second_set[2]])


def merge_all(stats, axis):
    size = lax.axis_size(axis)
    if is_power_of_two(size):
        for bit in range(size.bit_length() - 1):
            stats = merge_totals(stats, exchange(stats, axis, bit))
        return stats
    everything = lax.all_gather(stats, axis)
    return lax.fori_loop(1, size, lambda k, so_far: merge_totals(so_far, everything[k]), everything[0])


def body(
    dec_hidden,
    w_query,
    enc_states,
    w_out,
    norm_gain,
    w_vocab,
    enc_segment,
    dec_segment,
    seg_map,
    targets,
    loss_mask,
):
    dp_index = lax.axis_index("dp")
    fsdp_index = lax.axis_index("fsdp")
    dp_count = lax.axis_size("dp")
    fsdp_count = lax.axis_size("fsdp")
    dec_len, width = dec_hidden.shape
    enc_len = enc_states.shape[1]
    heads_here = w_query.shape[1] // HEAD_DIM
    segments = seg_map.shape[1]
    feature_count = width // fsdp_count
    vocab_here = w_vocab.shape[1]
    window = min(ENC_MOST, enc_len)
    split_fsdp = is_power_of_two(fsdp_count) and fsdp_count > 1
    levels = fsdp_count.bit_length() - 1

    rows = jnp.arange(dp_count)
    seg_ids = jnp.arange(segments)
    map_row = jnp.sum(jnp.where((rows == dp_index)[:, None], seg_map, 0), 0)
    sources = jnp.sum(
        jnp.where(dec_segment[:, None] == seg_ids[None, :], map_row[None, :], 0), 1
    )
    offsets = (seg_map[0] // segments) % dp_count
    hits = offsets[None, :] == rows[:, None]
    used = jnp.any(hits, 1)
    enc_rows = enc_segment.reshape(dp_count, enc_len)
    all_starts = jnp.sum(enc_rows[:, None, :] < seg_ids[None, :, None], 2)
    reader_hot = ((dp_index - rows) % dp_count)[:, None] == rows[None, :]
    reader_maps = jnp.sum(jnp.where(reader_hot[:, :, None], seg_map[None], 0), 1)
    send_seg = jnp.sum(jnp.where(hits, reader_maps, 0), 1) % segments
    my_starts = jnp.sum(jnp.where((rows == dp_index)[:, None], all_starts, 0), 0)
    send_start = jnp.clip(
        jnp.sum(jnp.where(send_seg[:, None] == seg_ids[None, :], my_starts[None, :], 0), 1),
        0,
        enc_len - window,
    )
    token_at = jnp.arange(enc_len)[None, None, :]
    send_pos = send_start[:, None] + jnp.arange(window)[None, :]
    pick = (token_at == send_pos[:, :, None]).astype(jnp.bfloat16)
    windows = jnp.einsum(
        "str,crf->sctf", pick, enc_states, preferred_element_type=jnp.float32
    ).astype(jnp.bfloat16)
    owner_hot = ((dp_index + rows) % dp_count)[:, None] == rows[None, :]
    owner_rows = jnp.sum(jnp.where(owner_hot[:, :, None], enc_rows[None], 0), 1)
    owner_starts = jnp.sum(jnp.where(owner_hot[:, :, None], all_starts[None], 0), 1)
    served = jnp.sum(jnp.where(hits, map_row[None, :], 0), 1)
    served_local = served % segments
    recv_start = jnp.clip(
        jnp.sum(jnp.where(served_local[:, None] == seg_ids[None, :], owner_starts, 0), 1),
        0,
        enc_len - window,
    )
    recv_pos = recv_start[:, None] + jnp.arange(window)[None, :]
    seg_at = jnp.sum(jnp.where(token_at == recv_pos[:, :, None], owner_rows[:, None, :], 0), 2)
    key_ids = jnp.where(used[:, None] & (seg_at == served_local[:, None]), served[:, None], -1)

    query_proj = jnp.dot(dec_hidden, w_query, preferred_element_type=jnp.float32).astype(
        jnp.bfloat16
    )
    queries = lax.optimization_barrier(query_proj).reshape(dec_len, heads_here, HEAD_DIM)
    run_sum = jnp.zeros((heads_here, dec_len), jnp.float32)
    run_acc = jnp.zeros((heads_here, dec_len, HEAD_DIM), jnp.float32)
    for shift in range(dp_count):
        block = windows[shift]
        if shift:
            block = lax.ppermute(
                block, "dp", [(i, (i - shift) % dp_count) for i in range(dp_count)]
            )
        keys_here = block[0].reshape(window, heads_here, HEAD_DIM)
        values_here = block[1].astype(jnp.float32).reshape(window, heads_here, HEAD_DIM)
        scores = jnp.einsum(
            "ihd,jhd->hij", queries, keys_here, preferred_element_type=jnp.float32
        )
        allowed = (sources[:, None] == key_ids[shift][None, :])[None]
        top = jnp.max(jnp.where(allowed, scores, jnp.float32(-1e30)), 2)
        weights = jnp.where(allowed, jnp.exp(scores - top[:, :, None]), 0.0)
        run_sum = run_sum + jnp.sum(weights, 2)
        run_acc = run_acc + jnp.einsum("hij,jhd->hid", weights, values_here)
    attended = (
        (run_acc / run_sum[:, :, None])
        .transpose(1, 0, 2)
        .reshape(dec_len, heads_here * HEAD_DIM)
        .astype(jnp.bfloat16)
    )

    feature_start = fsdp_index * feature_count
    gain_part = lax.dynamic_slice_in_dim(norm_gain, feature_start, feature_count, 0)
    hidden_part = lax.dynamic_slice_in_dim(dec_hidden, feature_start, feature_count, 1)
    projected = jnp.dot(attended, w_out, preferred_element_type=jnp.float32)
    if split_fsdp:
        projected = scatter_bits(projected, "fsdp", 1, levels, jnp.bfloat16)
    else:
        projected = lax.psum_scatter(projected, "fsdp", scatter_dimension=1, tiled=True)
    summed_part = projected + hidden_part.astype(jnp.float32)
    square_total = sum_all(jnp.sum(summed_part * summed_part, 1), "fsdp")
    inv_root = lax.rsqrt(square_total / width + 1e-06)
    unit_part = summed_part * inv_root[:, None]
    normed_part = (unit_part * gain_part).astype(jnp.bfloat16)
    if split_fsdp:
        half = width // 2
        top_side = (fsdp_index >> (levels - 1)) & 1
        near_rows = lax.dynamic_slice_in_dim(w_vocab, top_side * half, half, 0)
        far_rows = lax.dynamic_slice_in_dim(w_vocab, (1 - top_side) * half, half, 0)
        crossed = exchange(normed_part, "fsdp", levels - 1)
        near_normed = gather_bits(normed_part, "fsdp", 1, levels - 1)
        far_normed = gather_bits(crossed, "fsdp", 1, levels - 1)
        logits = jnp.dot(near_normed, near_rows, preferred_element_type=jnp.float32) + jnp.dot(
            far_normed, far_rows, preferred_element_type=jnp.float32
        )
    else:
        normed_full = lax.all_gather(normed_part, "fsdp", axis=1, tiled=True)
        logits = jnp.dot(normed_full, w_vocab, preferred_element_type=jnp.float32)
    local_target = targets - fsdp_index * vocab_here
    picked = jnp.arange(vocab_here)[None, :] == local_target[:, None]
    local_top = jnp.max(logits, 1)
    local_total = jnp.sum(jnp.exp(logits - local_top[:, None]), 1)
    local_pick = jnp.sum(jnp.where(picked, logits, 0.0), 1)
    row_top, row_total, target_logit = merge_all(
        jnp.stack([local_top, local_total, local_pick]), "fsdp"
    )
    log_total = row_top + jnp.log(row_total)
    mask_float = loss_mask.astype(jnp.float32)
    grad_logits = (
        mask_float[:, None] * (jnp.exp(logits - log_total[:, None]) - picked.astype(jnp.float32))
    ).astype(jnp.bfloat16)
    contract = (((1,), (1,)), ((), ()))
    if split_fsdp:
        far_grad = lax.dot_general(
            far_rows, grad_logits, contract, preferred_element_type=jnp.float32
        )
        far_grad, near_logits = lax.optimization_barrier(
            (scatter_bits(far_grad, "fsdp", 0, levels - 1), grad_logits)
        )
        far_grad = exchange(far_grad.astype(jnp.bfloat16), "fsdp", levels - 1).astype(
            jnp.float32
        )
        near_grad = lax.dot_general(
            near_rows, near_logits, contract, preferred_element_type=jnp.float32
        )
        grad_normed = (scatter_bits(near_grad, "fsdp", 0, levels - 1) + far_grad).T
    else:
        grad_normed = lax.psum_scatter(
            lax.dot_general(w_vocab, grad_logits, contract, preferred_element_type=jnp.float32),
            "fsdp",
            scatter_dimension=0,
            tiled=True,
        ).T
    grad_unit = grad_normed * gain_part
    inner_total = sum_all(jnp.sum(grad_unit * unit_part, 1), "fsdp")
    grad_summed = inv_root[:, None] * (grad_unit - unit_part * (inner_total / width)[:, None])
    gain_local = jnp.sum(grad_normed * unit_part, 0)
    packed = jnp.concatenate(
        [jnp.stack([jnp.sum(mask_float), jnp.sum(mask_float * (log_total - target_logit))]), gain_local]
    )
    packed = sum_all(packed, "dp")
    token_count, loss_total, gain_total = packed[0], packed[1], packed[2:]
    return (
        loss_total / token_count,
        (grad_summed / token_count).astype(jnp.bfloat16),
        gain_total / token_count,
    )


def solution(mesh):
    in_specs = (
        P("dp", None),
        P(None, "fsdp"),
        P(None, "dp", "fsdp"),
        P("fsdp", None),
        P(),
        P(None, "fsdp"),
        P(),
        P("dp"),
        P(),
        P("dp"),
        P("dp"),
    )
    out_specs = (P(), P("dp", "fsdp"), P("fsdp"))
    return jax.shard_map(body, mesh=mesh, in_specs=in_specs, out_specs=out_specs, check_vma=False)
```

```python
import jax
import jax.numpy as jnp
from jax import lax
from jax.sharding import PartitionSpec as P

HEAD_DIM = 64
ENC_MOST = 80


def is_power_of_two(n):
    return n & (n - 1) == 0


def exchange(x, axis, bit):
    size = lax.axis_size(axis)
    return lax.ppermute(x, axis, [(i, i ^ (1 << bit)) for i in range(size)])


def scatter_bits(x, axis, dim, levels, last_wire=None):
    me = lax.axis_index(axis)
    chunks = 1 << levels
    head, width, tail = x.shape[:dim], x.shape[dim] // chunks, x.shape[dim + 1 :]
    cur = x
    bit = 0
    while chunks > 1:
        cur = cur.reshape(head + (chunks // 2, 2, width) + tail)
        side = (me >> bit) & 1
        keep = lax.dynamic_index_in_dim(cur, side, dim + 1, keepdims=False)
        send = lax.dynamic_index_in_dim(cur, 1 - side, dim + 1, keepdims=False)
        if last_wire is not None and chunks == 2:
            cur = keep + exchange(send.astype(last_wire), axis, bit).astype(keep.dtype)
        else:
            cur = keep + exchange(send, axis, bit)
        chunks //= 2
        bit += 1
    return cur.reshape(head + (width,) + tail)


def gather_bits(x, axis, dim, levels):
    me = lax.axis_index(axis)
    head, width, tail = x.shape[:dim], x.shape[dim], x.shape[dim + 1 :]
    cur = x.reshape(head + (1, width) + tail)
    chunks = 1
    for bit in range(levels):
        got = exchange(cur, axis, bit)
        low = (me >> bit) & 1 == 0
        first = jnp.where(low, cur, got)
        second = jnp.where(low, got, cur)
        cur = jnp.stack([first, second], dim).reshape(head + (chunks * 2, width) + tail)
        chunks *= 2
    return cur.reshape(head + (chunks * width,) + tail)


def sum_all(x, axis):
    size = lax.axis_size(axis)
    if not is_power_of_two(size):
        return lax.psum(x, axis)
    for bit in range(size.bit_length() - 1):
        x = x + exchange(x, axis, bit)
    return x


def merge_totals(first_set, second_set):
    larger = jnp.maximum(first_set[0], second_set[0])
    combined = first_set[1] * jnp.exp(first_set[0] - larger) + second_set[1] * jnp.exp(
        second_set[0] - larger
    )
    return jnp.stack([larger, combined, first_set[2] + second_set[2]])


def merge_all(stats, axis):
    size = lax.axis_size(axis)
    if is_power_of_two(size):
        for bit in range(size.bit_length() - 1):
            stats = merge_totals(stats, exchange(stats, axis, bit))
        return stats
    everything = lax.all_gather(stats, axis)
    return lax.fori_loop(1, size, lambda k, so_far: merge_totals(so_far, everything[k]), everything[0])


def body(
    dec_hidden,
    w_query,
    enc_states,
    w_out,
    norm_gain,
    w_vocab,
    enc_segment,
    dec_segment,
    seg_map,
    targets,
    loss_mask,
):
    dp_index = lax.axis_index("dp")
    fsdp_index = lax.axis_index("fsdp")
    dp_count = lax.axis_size("dp")
    fsdp_count = lax.axis_size("fsdp")
    dec_len, width = dec_hidden.shape
    enc_len = enc_states.shape[1]
    heads_here = w_query.shape[1] // HEAD_DIM
    segments = seg_map.shape[1]
    feature_count = width // fsdp_count
    vocab_here = w_vocab.shape[1]
    window = min(ENC_MOST, enc_len)
    split_fsdp = is_power_of_two(fsdp_count) and fsdp_count > 1
    levels = fsdp_count.bit_length() - 1

    rows = jnp.arange(dp_count)
    seg_ids = jnp.arange(segments)
    map_row = jnp.sum(jnp.where((rows == dp_index)[:, None], seg_map, 0), 0)
    sources = jnp.sum(
        jnp.where(dec_segment[:, None] == seg_ids[None, :], map_row[None, :], 0), 1
    )
    offsets = (seg_map[0] // segments) % dp_count
    hits = offsets[None, :] == rows[:, None]
    used = jnp.any(hits, 1)
    enc_rows = enc_segment.reshape(dp_count, enc_len)
    all_starts = jnp.sum(enc_rows[:, None, :] < seg_ids[None, :, None], 2)
    reader_hot = ((dp_index - rows) % dp_count)[:, None] == rows[None, :]
    reader_maps = jnp.sum(jnp.where(reader_hot[:, :, None], seg_map[None], 0), 1)
    send_seg = jnp.sum(jnp.where(hits, reader_maps, 0), 1) % segments
    my_starts = jnp.sum(jnp.where((rows == dp_index)[:, None], all_starts, 0), 0)
    send_start = jnp.clip(
        jnp.sum(jnp.where(send_seg[:, None] == seg_ids[None, :], my_starts[None, :], 0), 1),
        0,
        enc_len - window,
    )
    token_at = jnp.arange(enc_len)[None, None, :]
    send_pos = send_start[:, None] + jnp.arange(window)[None, :]
    pick = (token_at == send_pos[:, :, None]).astype(jnp.bfloat16)
    windows = jnp.einsum(
        "str,crf->sctf", pick, enc_states, preferred_element_type=jnp.float32
    ).astype(jnp.bfloat16)
    owner_hot = ((dp_index + rows) % dp_count)[:, None] == rows[None, :]
    owner_rows = jnp.sum(jnp.where(owner_hot[:, :, None], enc_rows[None], 0), 1)
    owner_starts = jnp.sum(jnp.where(owner_hot[:, :, None], all_starts[None], 0), 1)
    served = jnp.sum(jnp.where(hits, map_row[None, :], 0), 1)
    served_local = served % segments
    recv_start = jnp.clip(
        jnp.sum(jnp.where(served_local[:, None] == seg_ids[None, :], owner_starts, 0), 1),
        0,
        enc_len - window,
    )
    recv_pos = recv_start[:, None] + jnp.arange(window)[None, :]
    seg_at = jnp.sum(jnp.where(token_at == recv_pos[:, :, None], owner_rows[:, None, :], 0), 2)
    key_ids = jnp.where(used[:, None] & (seg_at == served_local[:, None]), served[:, None], -1)

    query_proj = jnp.dot(dec_hidden, w_query, preferred_element_type=jnp.float32).astype(
        jnp.bfloat16
    )
    queries = lax.optimization_barrier(query_proj).reshape(dec_len, heads_here, HEAD_DIM)
    run_sum = jnp.zeros((heads_here, dec_len), jnp.float32)
    run_acc = jnp.zeros((heads_here, dec_len, HEAD_DIM), jnp.float32)
    for shift in range(dp_count):
        block = windows[shift]
        if shift:
            block = lax.ppermute(
                block, "dp", [(i, (i - shift) % dp_count) for i in range(dp_count)]
            )
        keys_here = block[0].reshape(window, heads_here, HEAD_DIM)
        values_here = block[1].astype(jnp.float32).reshape(window, heads_here, HEAD_DIM)
        scores = jnp.einsum(
            "ihd,jhd->hij", queries, keys_here, preferred_element_type=jnp.float32
        )
        allowed = (sources[:, None] == key_ids[shift][None, :])[None]
        top = jnp.max(jnp.where(allowed, scores, jnp.float32(-1e30)), 2)
        weights = jnp.where(allowed, jnp.exp(scores - top[:, :, None]), 0.0)
        run_sum = run_sum + jnp.sum(weights, 2)
        run_acc = run_acc + jnp.einsum("hij,jhd->hid", weights, values_here)
    attended = (
        (run_acc / run_sum[:, :, None])
        .transpose(1, 0, 2)
        .reshape(dec_len, heads_here * HEAD_DIM)
        .astype(jnp.bfloat16)
    )

    feature_start = fsdp_index * feature_count
    gain_part = lax.dynamic_slice_in_dim(norm_gain, feature_start, feature_count, 0)
    hidden_part = lax.dynamic_slice_in_dim(dec_hidden, feature_start, feature_count, 1)
    projected = jnp.dot(attended, w_out, preferred_element_type=jnp.float32)
    if split_fsdp:
        projected = scatter_bits(projected, "fsdp", 1, levels, jnp.bfloat16)
    else:
        projected = lax.psum_scatter(projected, "fsdp", scatter_dimension=1, tiled=True)
    summed_part = projected + hidden_part.astype(jnp.float32)
    square_total = sum_all(jnp.sum(summed_part * summed_part, 1), "fsdp")
    inv_root = lax.rsqrt(square_total / width + 1e-06)
    unit_part = summed_part * inv_root[:, None]
    normed_part = (summed_part * gain_part).astype(jnp.bfloat16)
    if split_fsdp:
        half = width // 2
        top_side = (fsdp_index >> (levels - 1)) & 1
        near_rows = lax.dynamic_slice_in_dim(w_vocab, top_side * half, half, 0)
        far_rows = lax.dynamic_slice_in_dim(w_vocab, (1 - top_side) * half, half, 0)
        near_normed = gather_bits(normed_part, "fsdp", 1, levels - 1)
        far_normed = exchange(near_normed, "fsdp", levels - 1)
        logits = (
            jnp.dot(near_normed, near_rows, preferred_element_type=jnp.float32)
            + jnp.dot(far_normed, far_rows, preferred_element_type=jnp.float32)
        ) * inv_root[:, None]
    else:
        normed_full = lax.all_gather(normed_part, "fsdp", axis=1, tiled=True)
        logits = jnp.dot(normed_full, w_vocab, preferred_element_type=jnp.float32) * inv_root[:, None]
    local_target = targets - fsdp_index * vocab_here
    picked = jnp.arange(vocab_here)[None, :] == local_target[:, None]
    local_top = jnp.max(logits, 1)
    local_total = jnp.sum(jnp.exp(logits - local_top[:, None]), 1)
    local_pick = jnp.sum(jnp.where(picked, logits, 0.0), 1)
    row_top, row_total, target_logit = merge_all(
        jnp.stack([local_top, local_total, local_pick]), "fsdp"
    )
    log_total = row_top + jnp.log(row_total)
    mask_float = loss_mask.astype(jnp.float32)
    grad_logits = (
        mask_float[:, None] * (jnp.exp(logits - log_total[:, None]) - picked.astype(jnp.float32))
    ).astype(jnp.bfloat16)
    contract = (((1,), (1,)), ((), ()))
    if split_fsdp:
        far_grad = lax.dot_general(
            far_rows, grad_logits, contract, preferred_element_type=jnp.float32
        )
        far_grad, near_logits = lax.optimization_barrier(
            (scatter_bits(far_grad, "fsdp", 0, levels - 1), grad_logits)
        )
        far_grad = exchange(far_grad.astype(jnp.bfloat16), "fsdp", levels - 1).astype(
            jnp.float32
        )
        near_grad = lax.dot_general(
            near_rows, near_logits, contract, preferred_element_type=jnp.float32
        )
        grad_normed = (scatter_bits(near_grad, "fsdp", 0, levels - 1) + far_grad).T
    else:
        grad_normed = lax.psum_scatter(
            lax.dot_general(w_vocab, grad_logits, contract, preferred_element_type=jnp.float32),
            "fsdp",
            scatter_dimension=0,
            tiled=True,
        ).T
    grad_unit = grad_normed * gain_part
    inner_total = sum_all(jnp.sum(grad_unit * unit_part, 1), "fsdp")
    grad_summed = inv_root[:, None] * (grad_unit - unit_part * (inner_total / width)[:, None])
    gain_local = jnp.sum(grad_normed * unit_part, 0)
    packed = jnp.concatenate(
        [jnp.stack([jnp.sum(mask_float), jnp.sum(mask_float * (log_total - target_logit))]), gain_local]
    )
    packed = sum_all(packed, "dp")
    token_count, loss_total, gain_total = packed[0], packed[1], packed[2:]
    return (
        loss_total / token_count,
        (grad_summed / token_count).astype(jnp.bfloat16),
        gain_total / token_count,
    )


def solution(mesh):
    in_specs = (
        P("dp", None),
        P(None, "fsdp"),
        P(None, "dp", "fsdp"),
        P("fsdp", None),
        P(),
        P(None, "fsdp"),
        P(),
        P("dp"),
        P(),
        P("dp"),
        P("dp"),
    )
    out_specs = (P(), P("dp", "fsdp"), P("fsdp"))
    return jax.shard_map(body, mesh=mesh, in_specs=in_specs, out_specs=out_specs, check_vma=False)
```

```python
import jax
import jax.numpy as jnp
from jax import lax
from jax.sharding import PartitionSpec as P

HEAD_DIM = 64
ENC_MOST = 80


def is_power_of_two(n):
    return n & (n - 1) == 0


def exchange(x, axis, bit):
    size = lax.axis_size(axis)
    return lax.ppermute(x, axis, [(i, i ^ (1 << bit)) for i in range(size)])


def scatter_bits(x, axis, dim, levels, last_wire=None):
    me = lax.axis_index(axis)
    chunks = 1 << levels
    head, width, tail = x.shape[:dim], x.shape[dim] // chunks, x.shape[dim + 1 :]
    cur = x
    bit = 0
    while chunks > 1:
        cur = cur.reshape(head + (chunks // 2, 2, width) + tail)
        side = (me >> bit) & 1
        keep = lax.dynamic_index_in_dim(cur, side, dim + 1, keepdims=False)
        send = lax.dynamic_index_in_dim(cur, 1 - side, dim + 1, keepdims=False)
        if last_wire is not None and chunks == 2:
            cur = keep + exchange(send.astype(last_wire), axis, bit).astype(keep.dtype)
        else:
            cur = keep + exchange(send, axis, bit)
        chunks //= 2
        bit += 1
    return cur.reshape(head + (width,) + tail)


def gather_bits(x, axis, dim, levels):
    me = lax.axis_index(axis)
    head, width, tail = x.shape[:dim], x.shape[dim], x.shape[dim + 1 :]
    cur = x.reshape(head + (1, width) + tail)
    chunks = 1
    for bit in range(levels):
        got = exchange(cur, axis, bit)
        low = (me >> bit) & 1 == 0
        first = jnp.where(low, cur, got)
        second = jnp.where(low, got, cur)
        cur = jnp.stack([first, second], dim).reshape(head + (chunks * 2, width) + tail)
        chunks *= 2
    return cur.reshape(head + (chunks * width,) + tail)


def sum_all(x, axis):
    size = lax.axis_size(axis)
    if not is_power_of_two(size):
        return lax.psum(x, axis)
    for bit in range(size.bit_length() - 1):
        x = x + exchange(x, axis, bit)
    return x


def merge_totals(first_set, second_set):
    larger = jnp.maximum(first_set[0], second_set[0])
    combined = first_set[1] * jnp.exp(first_set[0] - larger) + second_set[1] * jnp.exp(
        second_set[0] - larger
    )
    return jnp.stack([larger, combined, first_set[2] + second_set[2]])


def merge_all(stats, axis):
    size = lax.axis_size(axis)
    if is_power_of_two(size):
        for bit in range(size.bit_length() - 1):
            stats = merge_totals(stats, exchange(stats, axis, bit))
        return stats
    everything = lax.all_gather(stats, axis)
    return lax.fori_loop(1, size, lambda k, so_far: merge_totals(so_far, everything[k]), everything[0])


def body(
    dec_hidden,
    w_query,
    enc_states,
    w_out,
    norm_gain,
    w_vocab,
    enc_segment,
    dec_segment,
    seg_map,
    targets,
    loss_mask,
):
    dp_index = lax.axis_index("dp")
    fsdp_index = lax.axis_index("fsdp")
    dp_count = lax.axis_size("dp")
    fsdp_count = lax.axis_size("fsdp")
    dec_len, width = dec_hidden.shape
    enc_len = enc_states.shape[1]
    heads_here = w_query.shape[1] // HEAD_DIM
    segments = seg_map.shape[1]
    feature_count = width // fsdp_count
    vocab_here = w_vocab.shape[1]
    window = min(ENC_MOST, enc_len)
    split_fsdp = is_power_of_two(fsdp_count) and fsdp_count > 1
    levels = fsdp_count.bit_length() - 1

    rows = jnp.arange(dp_count)
    seg_ids = jnp.arange(segments)
    map_row = jnp.sum(jnp.where((rows == dp_index)[:, None], seg_map, 0), 0)
    sources = jnp.sum(
        jnp.where(dec_segment[:, None] == seg_ids[None, :], map_row[None, :], 0), 1
    )
    offsets = (seg_map[0] // segments) % dp_count
    hits = offsets[None, :] == rows[:, None]
    used = jnp.any(hits, 1)
    enc_rows = enc_segment.reshape(dp_count, enc_len)
    all_starts = jnp.sum(enc_rows[:, None, :] < seg_ids[None, :, None], 2)
    reader_hot = ((dp_index - rows) % dp_count)[:, None] == rows[None, :]
    reader_maps = jnp.sum(jnp.where(reader_hot[:, :, None], seg_map[None], 0), 1)
    send_seg = jnp.sum(jnp.where(hits, reader_maps, 0), 1) % segments
    my_starts = jnp.sum(jnp.where((rows == dp_index)[:, None], all_starts, 0), 0)
    send_start = jnp.clip(
        jnp.sum(jnp.where(send_seg[:, None] == seg_ids[None, :], my_starts[None, :], 0), 1),
        0,
        enc_len - window,
    )
    token_at = jnp.arange(enc_len)[None, None, :]
    send_pos = send_start[:, None] + jnp.arange(window)[None, :]
    pick = (token_at == send_pos[:, :, None]).astype(jnp.bfloat16)
    windows = jnp.einsum(
        "str,crf->sctf", pick, enc_states, preferred_element_type=jnp.float32
    ).astype(jnp.bfloat16)
    owner_hot = ((dp_index + rows) % dp_count)[:, None] == rows[None, :]
    owner_rows = jnp.sum(jnp.where(owner_hot[:, :, None], enc_rows[None], 0), 1)
    owner_starts = jnp.sum(jnp.where(owner_hot[:, :, None], all_starts[None], 0), 1)
    served = jnp.sum(jnp.where(hits, map_row[None, :], 0), 1)
    served_local = served % segments
    recv_start = jnp.clip(
        jnp.sum(jnp.where(served_local[:, None] == seg_ids[None, :], owner_starts, 0), 1),
        0,
        enc_len - window,
    )
    recv_pos = recv_start[:, None] + jnp.arange(window)[None, :]
    seg_at = jnp.sum(jnp.where(token_at == recv_pos[:, :, None], owner_rows[:, None, :], 0), 2)
    key_ids = jnp.where(used[:, None] & (seg_at == served_local[:, None]), served[:, None], -1)

    query_proj = jnp.dot(dec_hidden, w_query, preferred_element_type=jnp.float32).astype(
        jnp.bfloat16
    )
    queries = lax.optimization_barrier(query_proj)
    head_mask = jnp.arange(heads_here)[:, None] == jnp.arange(heads_here * HEAD_DIM)[None, :] // HEAD_DIM
    spread = jnp.where(head_mask[:, None, :], queries[None], jnp.zeros((), queries.dtype)).reshape(
        heads_here * dec_len, heads_here * HEAD_DIM
    )
    spread_sources = jnp.tile(sources, heads_here)
    run_sum = jnp.zeros((heads_here * dec_len,), jnp.float32)
    run_acc = jnp.zeros((heads_here * dec_len, heads_here * HEAD_DIM), jnp.float32)
    for shift in range(dp_count):
        block = windows[shift]
        if shift:
            block = lax.ppermute(
                block, "dp", [(i, (i - shift) % dp_count) for i in range(dp_count)]
            )
        scores = lax.dot_general(
            spread, block[0], (((1,), (1,)), ((), ())), preferred_element_type=jnp.float32
        )
        allowed = spread_sources[:, None] == key_ids[shift][None, :]
        top = jnp.max(jnp.where(allowed, scores, jnp.float32(-1e30)), 1)
        weights = jnp.where(allowed, jnp.exp(scores - top[:, None]), 0.0)
        run_sum = run_sum + jnp.sum(weights, 1)
        run_acc = run_acc + jnp.dot(weights, block[1].astype(jnp.float32))
    spread_out = (run_acc / run_sum[:, None]).reshape(heads_here, dec_len, heads_here * HEAD_DIM)
    attended = jnp.sum(jnp.where(head_mask[:, None, :], spread_out, 0.0), 0).astype(jnp.bfloat16)

    feature_start = fsdp_index * feature_count
    gain_part = lax.dynamic_slice_in_dim(norm_gain, feature_start, feature_count, 0)
    hidden_part = lax.dynamic_slice_in_dim(dec_hidden, feature_start, feature_count, 1)
    projected = jnp.dot(attended, w_out, preferred_element_type=jnp.float32)
    if split_fsdp:
        projected = scatter_bits(projected, "fsdp", 1, levels, jnp.bfloat16)
    else:
        projected = lax.psum_scatter(projected, "fsdp", scatter_dimension=1, tiled=True)
    summed_part = projected + hidden_part.astype(jnp.float32)
    square_total = sum_all(jnp.sum(summed_part * summed_part, 1), "fsdp")
    inv_root = lax.rsqrt(square_total / width + 1e-06)
    unit_part = summed_part * inv_root[:, None]
    normed_part = (summed_part * gain_part).astype(jnp.bfloat16)
    if split_fsdp:
        half = width // 2
        top_side = (fsdp_index >> (levels - 1)) & 1
        near_rows = lax.dynamic_slice_in_dim(w_vocab, top_side * half, half, 0)
        far_rows = lax.dynamic_slice_in_dim(w_vocab, (1 - top_side) * half, half, 0)
        near_normed = gather_bits(normed_part, "fsdp", 1, levels - 1)
        far_normed = exchange(near_normed, "fsdp", levels - 1)
        logits = (
            jnp.dot(near_normed, near_rows, preferred_element_type=jnp.float32)
            + jnp.dot(far_normed, far_rows, preferred_element_type=jnp.float32)
        ) * inv_root[:, None]
    else:
        normed_full = lax.all_gather(normed_part, "fsdp", axis=1, tiled=True)
        logits = jnp.dot(normed_full, w_vocab, preferred_element_type=jnp.float32) * inv_root[:, None]
    local_target = targets - fsdp_index * vocab_here
    picked = jnp.arange(vocab_here)[None, :] == local_target[:, None]
    local_top = jnp.max(logits, 1)
    local_total = jnp.sum(jnp.exp(logits - local_top[:, None]), 1)
    local_pick = jnp.sum(jnp.where(picked, logits, 0.0), 1)
    row_top, row_total, target_logit = merge_all(
        jnp.stack([local_top, local_total, local_pick]), "fsdp"
    )
    log_total = row_top + jnp.log(row_total)
    mask_float = loss_mask.astype(jnp.float32)
    grad_logits = (
        mask_float[:, None] * (jnp.exp(logits - log_total[:, None]) - picked.astype(jnp.float32))
    ).astype(jnp.bfloat16)
    contract = (((1,), (1,)), ((), ()))
    if split_fsdp:
        far_grad = lax.dot_general(
            far_rows, grad_logits, contract, preferred_element_type=jnp.float32
        )
        far_grad, near_logits = lax.optimization_barrier(
            (scatter_bits(far_grad, "fsdp", 0, levels - 1), grad_logits)
        )
        far_grad = exchange(far_grad.astype(jnp.bfloat16), "fsdp", levels - 1).astype(
            jnp.float32
        )
        near_grad = lax.dot_general(
            near_rows, near_logits, contract, preferred_element_type=jnp.float32
        )
        grad_normed = (scatter_bits(near_grad, "fsdp", 0, levels - 1) + far_grad).T
    else:
        grad_normed = lax.psum_scatter(
            lax.dot_general(w_vocab, grad_logits, contract, preferred_element_type=jnp.float32),
            "fsdp",
            scatter_dimension=0,
            tiled=True,
        ).T
    grad_unit = grad_normed * gain_part
    inner_total = sum_all(jnp.sum(grad_unit * unit_part, 1), "fsdp")
    grad_summed = inv_root[:, None] * (grad_unit - unit_part * (inner_total / width)[:, None])
    gain_local = jnp.sum(grad_normed * unit_part, 0)
    packed = jnp.concatenate(
        [jnp.stack([jnp.sum(mask_float), jnp.sum(mask_float * (log_total - target_logit))]), gain_local]
    )
    packed = sum_all(packed, "dp")
    token_count, loss_total, gain_total = packed[0], packed[1], packed[2:]
    return (
        loss_total / token_count,
        (grad_summed / token_count).astype(jnp.bfloat16),
        gain_total / token_count,
    )


def solution(mesh):
    in_specs = (
        P("dp", None),
        P(None, "fsdp"),
        P(None, "dp", "fsdp"),
        P("fsdp", None),
        P(),
        P(None, "fsdp"),
        P(),
        P("dp"),
        P(),
        P("dp"),
        P("dp"),
    )
    out_specs = (P(), P("dp", "fsdp"), P("fsdp"))
    return jax.shard_map(body, mesh=mesh, in_specs=in_specs, out_specs=out_specs, check_vma=False)
```

```python
import jax
import jax.numpy as jnp
from jax import lax
from jax.sharding import PartitionSpec as P

HEAD_DIM = 64
ENC_MOST = 80


def is_power_of_two(n):
    return n & (n - 1) == 0


def exchange(x, axis, bit):
    size = lax.axis_size(axis)
    return lax.ppermute(x, axis, [(i, i ^ (1 << bit)) for i in range(size)])


def scatter_bits(x, axis, dim, levels, last_wire=None):
    me = lax.axis_index(axis)
    chunks = 1 << levels
    head, width, tail = x.shape[:dim], x.shape[dim] // chunks, x.shape[dim + 1 :]
    cur = x
    bit = 0
    while chunks > 1:
        cur = cur.reshape(head + (chunks // 2, 2, width) + tail)
        side = (me >> bit) & 1
        keep = lax.dynamic_index_in_dim(cur, side, dim + 1, keepdims=False)
        send = lax.dynamic_index_in_dim(cur, 1 - side, dim + 1, keepdims=False)
        if last_wire is not None and chunks == 2:
            cur = keep + exchange(send.astype(last_wire), axis, bit).astype(keep.dtype)
        else:
            cur = keep + exchange(send, axis, bit)
        chunks //= 2
        bit += 1
    return cur.reshape(head + (width,) + tail)


def gather_bits(x, axis, dim, levels):
    me = lax.axis_index(axis)
    head, width, tail = x.shape[:dim], x.shape[dim], x.shape[dim + 1 :]
    cur = x.reshape(head + (1, width) + tail)
    chunks = 1
    for bit in range(levels):
        got = exchange(cur, axis, bit)
        low = (me >> bit) & 1 == 0
        first = jnp.where(low, cur, got)
        second = jnp.where(low, got, cur)
        cur = jnp.stack([first, second], dim).reshape(head + (chunks * 2, width) + tail)
        chunks *= 2
    return cur.reshape(head + (chunks * width,) + tail)


def sum_all(x, axis):
    size = lax.axis_size(axis)
    if not is_power_of_two(size):
        return lax.psum(x, axis)
    for bit in range(size.bit_length() - 1):
        x = x + exchange(x, axis, bit)
    return x


def merge_totals(first_set, second_set):
    larger = jnp.maximum(first_set[0], second_set[0])
    combined = first_set[1] * jnp.exp(first_set[0] - larger) + second_set[1] * jnp.exp(
        second_set[0] - larger
    )
    return jnp.stack([larger, combined, first_set[2] + second_set[2]])


def merge_all(stats, axis):
    size = lax.axis_size(axis)
    if is_power_of_two(size):
        for bit in range(size.bit_length() - 1):
            stats = merge_totals(stats, exchange(stats, axis, bit))
        return stats
    everything = lax.all_gather(stats, axis)
    return lax.fori_loop(1, size, lambda k, so_far: merge_totals(so_far, everything[k]), everything[0])


def body(
    dec_hidden,
    w_query,
    enc_states,
    w_out,
    norm_gain,
    w_vocab,
    enc_segment,
    dec_segment,
    seg_map,
    targets,
    loss_mask,
):
    dp_index = lax.axis_index("dp")
    fsdp_index = lax.axis_index("fsdp")
    dp_count = lax.axis_size("dp")
    fsdp_count = lax.axis_size("fsdp")
    dec_len, width = dec_hidden.shape
    enc_len = enc_states.shape[1]
    heads_here = w_query.shape[1] // HEAD_DIM
    segments = seg_map.shape[1]
    feature_count = width // fsdp_count
    vocab_here = w_vocab.shape[1]
    window = min(ENC_MOST, enc_len)
    split_fsdp = is_power_of_two(fsdp_count) and fsdp_count > 1
    levels = fsdp_count.bit_length() - 1

    rows = jnp.arange(dp_count)
    seg_ids = jnp.arange(segments)
    map_row = jnp.sum(jnp.where((rows == dp_index)[:, None], seg_map, 0), 0)
    sources = jnp.sum(
        jnp.where(dec_segment[:, None] == seg_ids[None, :], map_row[None, :], 0), 1
    )
    offsets = (seg_map[0] // segments) % dp_count
    hits = offsets[None, :] == rows[:, None]
    used = jnp.any(hits, 1)
    enc_rows = enc_segment.reshape(dp_count, enc_len)
    all_starts = jnp.sum(enc_rows[:, None, :] < seg_ids[None, :, None], 2)
    reader_hot = ((dp_index - rows) % dp_count)[:, None] == rows[None, :]
    reader_maps = jnp.sum(jnp.where(reader_hot[:, :, None], seg_map[None], 0), 1)
    send_seg = jnp.sum(jnp.where(hits, reader_maps, 0), 1) % segments
    my_starts = jnp.sum(jnp.where((rows == dp_index)[:, None], all_starts, 0), 0)
    send_start = jnp.clip(
        jnp.sum(jnp.where(send_seg[:, None] == seg_ids[None, :], my_starts[None, :], 0), 1),
        0,
        enc_len - window,
    )
    token_at = jnp.arange(enc_len)[None, None, :]
    send_pos = send_start[:, None] + jnp.arange(window)[None, :]
    pick = (token_at == send_pos[:, :, None]).astype(jnp.bfloat16)
    windows = jnp.einsum(
        "str,crf->sctf", pick, enc_states, preferred_element_type=jnp.float32
    ).astype(jnp.bfloat16)
    owner_hot = ((dp_index + rows) % dp_count)[:, None] == rows[None, :]
    owner_rows = jnp.sum(jnp.where(owner_hot[:, :, None], enc_rows[None], 0), 1)
    owner_starts = jnp.sum(jnp.where(owner_hot[:, :, None], all_starts[None], 0), 1)
    served = jnp.sum(jnp.where(hits, map_row[None, :], 0), 1)
    served_local = served % segments
    recv_start = jnp.clip(
        jnp.sum(jnp.where(served_local[:, None] == seg_ids[None, :], owner_starts, 0), 1),
        0,
        enc_len - window,
    )
    recv_pos = recv_start[:, None] + jnp.arange(window)[None, :]
    seg_at = jnp.sum(jnp.where(token_at == recv_pos[:, :, None], owner_rows[:, None, :], 0), 2)
    key_ids = jnp.where(used[:, None] & (seg_at == served_local[:, None]), served[:, None], -1)

    query_proj = jnp.dot(dec_hidden, w_query, preferred_element_type=jnp.float32).astype(
        jnp.bfloat16
    )
    queries = lax.optimization_barrier(query_proj).reshape(dec_len, heads_here, HEAD_DIM)
    run_sum = jnp.zeros((heads_here, dec_len), jnp.float32)
    run_acc = jnp.zeros((heads_here, dec_len, HEAD_DIM), jnp.float32)
    for shift in range(dp_count):
        block = windows[shift]
        if shift:
            block = lax.ppermute(
                block, "dp", [(i, (i - shift) % dp_count) for i in range(dp_count)]
            )
        keys_here = block[0].reshape(window, heads_here, HEAD_DIM)
        values_here = block[1].astype(jnp.float32).reshape(window, heads_here, HEAD_DIM)
        scores = jnp.einsum(
            "ihd,jhd->hij", queries, keys_here, preferred_element_type=jnp.float32
        )
        allowed = (sources[:, None] == key_ids[shift][None, :])[None]
        top = jnp.max(jnp.where(allowed, scores, jnp.float32(-1e30)), 2)
        weights = jnp.where(allowed, jnp.exp(scores - top[:, :, None]), 0.0)
        run_sum = run_sum + jnp.sum(weights, 2)
        run_acc = run_acc + jnp.einsum("hij,jhd->hid", weights, values_here)
    attended = (
        (run_acc / run_sum[:, :, None])
        .transpose(1, 0, 2)
        .reshape(dec_len, heads_here * HEAD_DIM)
        .astype(jnp.bfloat16)
    )

    feature_start = fsdp_index * feature_count
    gain_part = lax.dynamic_slice_in_dim(norm_gain, feature_start, feature_count, 0)
    hidden_part = lax.dynamic_slice_in_dim(dec_hidden, feature_start, feature_count, 1)
    if levels == 2:
        quarter = width // 4
        low_bit, high_bit = fsdp_index & 1, fsdp_index >> 1

        def chunk_product(chunk):
            columns = lax.dynamic_slice_in_dim(w_out, chunk * quarter, quarter, 1)
            return jnp.dot(attended, columns, preferred_element_type=jnp.float32)

        sent = jnp.stack([chunk_product(1 - low_bit), chunk_product(3 - low_bit)])
        kept = jnp.stack([chunk_product(low_bit), chunk_product(2 + low_bit)])
        kept = kept + exchange(sent, "fsdp", 0)
        mine = lax.dynamic_index_in_dim(kept, high_bit, 0, keepdims=False)
        other = lax.dynamic_index_in_dim(kept, 1 - high_bit, 0, keepdims=False)
        projected = mine + exchange(other.astype(jnp.bfloat16), "fsdp", 1).astype(jnp.float32)
    elif split_fsdp:
        projected = jnp.dot(attended, w_out, preferred_element_type=jnp.float32)
        projected = scatter_bits(projected, "fsdp", 1, levels, jnp.bfloat16)
    else:
        projected = jnp.dot(attended, w_out, preferred_element_type=jnp.float32)
        projected = lax.psum_scatter(projected, "fsdp", scatter_dimension=1, tiled=True)
    summed_part = projected + hidden_part.astype(jnp.float32)
    square_total = sum_all(jnp.sum(summed_part * summed_part, 1), "fsdp")
    inv_root = lax.rsqrt(square_total / width + 1e-06)
    unit_part = summed_part * inv_root[:, None]
    normed_part = (summed_part * gain_part).astype(jnp.bfloat16)
    if split_fsdp:
        half = width // 2
        top_side = (fsdp_index >> (levels - 1)) & 1
        near_rows = lax.dynamic_slice_in_dim(w_vocab, top_side * half, half, 0)
        far_rows = lax.dynamic_slice_in_dim(w_vocab, (1 - top_side) * half, half, 0)
        near_normed = gather_bits(normed_part, "fsdp", 1, levels - 1)
        far_normed = exchange(near_normed, "fsdp", levels - 1)
        logits = (
            jnp.dot(near_normed, near_rows, preferred_element_type=jnp.float32)
            + jnp.dot(far_normed, far_rows, preferred_element_type=jnp.float32)
        ) * inv_root[:, None]
    else:
        normed_full = lax.all_gather(normed_part, "fsdp", axis=1, tiled=True)
        logits = jnp.dot(normed_full, w_vocab, preferred_element_type=jnp.float32) * inv_root[:, None]
    local_target = targets - fsdp_index * vocab_here
    picked = jnp.arange(vocab_here)[None, :] == local_target[:, None]
    local_top = jnp.max(logits, 1)
    local_total = jnp.sum(jnp.exp(logits - local_top[:, None]), 1)
    local_pick = jnp.sum(jnp.where(picked, logits, 0.0), 1)
    row_top, row_total, target_logit = merge_all(
        jnp.stack([local_top, local_total, local_pick]), "fsdp"
    )
    log_total = row_top + jnp.log(row_total)
    mask_float = loss_mask.astype(jnp.float32)
    grad_logits = (
        mask_float[:, None] * (jnp.exp(logits - log_total[:, None]) - picked.astype(jnp.float32))
    ).astype(jnp.bfloat16)
    contract = (((1,), (1,)), ((), ()))
    if split_fsdp:
        far_grad = lax.dot_general(
            far_rows, grad_logits, contract, preferred_element_type=jnp.float32
        )
        far_grad, near_logits = lax.optimization_barrier(
            (scatter_bits(far_grad, "fsdp", 0, levels - 1), grad_logits)
        )
        far_grad = exchange(far_grad.astype(jnp.bfloat16), "fsdp", levels - 1).astype(
            jnp.float32
        )
        near_grad = lax.dot_general(
            near_rows, near_logits, contract, preferred_element_type=jnp.float32
        )
        grad_normed = (scatter_bits(near_grad, "fsdp", 0, levels - 1) + far_grad).T
    else:
        grad_normed = lax.psum_scatter(
            lax.dot_general(w_vocab, grad_logits, contract, preferred_element_type=jnp.float32),
            "fsdp",
            scatter_dimension=0,
            tiled=True,
        ).T
    grad_unit = grad_normed * gain_part
    inner_total = sum_all(jnp.sum(grad_unit * unit_part, 1), "fsdp")
    grad_summed = inv_root[:, None] * (grad_unit - unit_part * (inner_total / width)[:, None])
    gain_local = jnp.sum(grad_normed * unit_part, 0)
    packed = jnp.concatenate(
        [jnp.stack([jnp.sum(mask_float), jnp.sum(mask_float * (log_total - target_logit))]), gain_local]
    )
    packed = sum_all(packed, "dp")
    token_count, loss_total, gain_total = packed[0], packed[1], packed[2:]
    return (
        loss_total / token_count,
        (grad_summed / token_count).astype(jnp.bfloat16),
        gain_total / token_count,
    )


def solution(mesh):
    in_specs = (
        P("dp", None),
        P(None, "fsdp"),
        P(None, "dp", "fsdp"),
        P("fsdp", None),
        P(),
        P(None, "fsdp"),
        P(),
        P("dp"),
        P(),
        P("dp"),
        P("dp"),
    )
    out_specs = (P(), P("dp", "fsdp"), P("fsdp"))
    return jax.shard_map(body, mesh=mesh, in_specs=in_specs, out_specs=out_specs, check_vma=False)
```

```python
import jax
import jax.numpy as jnp
from jax import lax
from jax.sharding import PartitionSpec as P

HEAD_DIM = 64
ENC_MOST = 80


def is_power_of_two(n):
    return n & (n - 1) == 0


def exchange(x, axis, bit):
    size = lax.axis_size(axis)
    return lax.ppermute(x, axis, [(i, i ^ (1 << bit)) for i in range(size)])


def scatter_bits(x, axis, dim, levels, last_wire=None):
    me = lax.axis_index(axis)
    chunks = 1 << levels
    head, width, tail = x.shape[:dim], x.shape[dim] // chunks, x.shape[dim + 1 :]
    cur = x
    bit = 0
    while chunks > 1:
        cur = cur.reshape(head + (chunks // 2, 2, width) + tail)
        side = (me >> bit) & 1
        keep = lax.dynamic_index_in_dim(cur, side, dim + 1, keepdims=False)
        send = lax.dynamic_index_in_dim(cur, 1 - side, dim + 1, keepdims=False)
        if last_wire is not None and chunks == 2:
            cur = keep + exchange(send.astype(last_wire), axis, bit).astype(keep.dtype)
        else:
            cur = keep + exchange(send, axis, bit)
        chunks //= 2
        bit += 1
    return cur.reshape(head + (width,) + tail)


def gather_bits(x, axis, dim, levels):
    me = lax.axis_index(axis)
    head, width, tail = x.shape[:dim], x.shape[dim], x.shape[dim + 1 :]
    cur = x.reshape(head + (1, width) + tail)
    chunks = 1
    for bit in range(levels):
        got = exchange(cur, axis, bit)
        low = (me >> bit) & 1 == 0
        first = jnp.where(low, cur, got)
        second = jnp.where(low, got, cur)
        cur = jnp.stack([first, second], dim).reshape(head + (chunks * 2, width) + tail)
        chunks *= 2
    return cur.reshape(head + (chunks * width,) + tail)


def sum_all(x, axis):
    size = lax.axis_size(axis)
    if not is_power_of_two(size):
        return lax.psum(x, axis)
    for bit in range(size.bit_length() - 1):
        x = x + exchange(x, axis, bit)
    return x


def merge_totals(first_set, second_set):
    larger = jnp.maximum(first_set[0], second_set[0])
    combined = first_set[1] * jnp.exp(first_set[0] - larger) + second_set[1] * jnp.exp(
        second_set[0] - larger
    )
    return jnp.stack([larger, combined, first_set[2] + second_set[2]])


def merge_all(stats, axis):
    size = lax.axis_size(axis)
    if is_power_of_two(size):
        for bit in range(size.bit_length() - 1):
            stats = merge_totals(stats, exchange(stats, axis, bit))
        return stats
    everything = lax.all_gather(stats, axis)
    return lax.fori_loop(1, size, lambda k, so_far: merge_totals(so_far, everything[k]), everything[0])


def body(
    dec_hidden,
    w_query,
    enc_states,
    w_out,
    norm_gain,
    w_vocab,
    enc_segment,
    dec_segment,
    seg_map,
    targets,
    loss_mask,
):
    dp_index = lax.axis_index("dp")
    fsdp_index = lax.axis_index("fsdp")
    dp_count = lax.axis_size("dp")
    fsdp_count = lax.axis_size("fsdp")
    dec_len, width = dec_hidden.shape
    enc_len = enc_states.shape[1]
    heads_here = w_query.shape[1] // HEAD_DIM
    segments = seg_map.shape[1]
    feature_count = width // fsdp_count
    vocab_here = w_vocab.shape[1]
    window = min(ENC_MOST, enc_len)
    split_fsdp = is_power_of_two(fsdp_count) and fsdp_count > 1
    levels = fsdp_count.bit_length() - 1

    rows = jnp.arange(dp_count)
    seg_ids = jnp.arange(segments)
    map_row = jnp.sum(jnp.where((rows == dp_index)[:, None], seg_map, 0), 0)
    sources = jnp.sum(
        jnp.where(dec_segment[:, None] == seg_ids[None, :], map_row[None, :], 0), 1
    )
    offsets = (seg_map[0] // segments) % dp_count
    hits = offsets[None, :] == rows[:, None]
    used = jnp.any(hits, 1)
    enc_rows = enc_segment.reshape(dp_count, enc_len)
    all_starts = jnp.sum(enc_rows[:, None, :] < seg_ids[None, :, None], 2)
    reader_hot = ((dp_index - rows) % dp_count)[:, None] == rows[None, :]
    reader_maps = jnp.sum(jnp.where(reader_hot[:, :, None], seg_map[None], 0), 1)
    send_seg = jnp.sum(jnp.where(hits, reader_maps, 0), 1) % segments
    my_starts = jnp.sum(jnp.where((rows == dp_index)[:, None], all_starts, 0), 0)
    send_start = jnp.clip(
        jnp.sum(jnp.where(send_seg[:, None] == seg_ids[None, :], my_starts[None, :], 0), 1),
        0,
        enc_len - window,
    )
    token_at = jnp.arange(enc_len)[None, None, :]
    send_pos = send_start[:, None] + jnp.arange(window)[None, :]
    pick = (token_at == send_pos[:, :, None]).astype(jnp.bfloat16)
    windows = jnp.einsum(
        "str,crf->sctf", pick, enc_states, preferred_element_type=jnp.float32
    ).astype(jnp.bfloat16)
    owner_hot = ((dp_index + rows) % dp_count)[:, None] == rows[None, :]
    owner_rows = jnp.sum(jnp.where(owner_hot[:, :, None], enc_rows[None], 0), 1)
    owner_starts = jnp.sum(jnp.where(owner_hot[:, :, None], all_starts[None], 0), 1)
    served = jnp.sum(jnp.where(hits, map_row[None, :], 0), 1)
    served_local = served % segments
    recv_start = jnp.clip(
        jnp.sum(jnp.where(served_local[:, None] == seg_ids[None, :], owner_starts, 0), 1),
        0,
        enc_len - window,
    )
    recv_pos = recv_start[:, None] + jnp.arange(window)[None, :]
    seg_at = jnp.sum(jnp.where(token_at == recv_pos[:, :, None], owner_rows[:, None, :], 0), 2)
    key_ids = jnp.where(used[:, None] & (seg_at == served_local[:, None]), served[:, None], -1)

    query_proj = jnp.dot(dec_hidden, w_query, preferred_element_type=jnp.float32).astype(
        jnp.bfloat16
    )
    queries = lax.optimization_barrier(query_proj).reshape(dec_len, heads_here, HEAD_DIM)
    run_sum = jnp.zeros((heads_here, dec_len), jnp.float32)
    run_acc = jnp.zeros((heads_here, dec_len, HEAD_DIM), jnp.float32)
    for shift in range(dp_count):
        block = windows[shift]
        if shift:
            block = lax.ppermute(
                block, "dp", [(i, (i - shift) % dp_count) for i in range(dp_count)]
            )
        keys_here = block[0].reshape(window, heads_here, HEAD_DIM)
        values_here = block[1].astype(jnp.float32).reshape(window, heads_here, HEAD_DIM)
        scores = jnp.einsum(
            "ihd,jhd->hij", queries, keys_here, preferred_element_type=jnp.float32
        )
        allowed = (sources[:, None] == key_ids[shift][None, :])[None]
        top = jnp.max(jnp.where(allowed, scores, jnp.float32(-1e30)), 2)
        weights = jnp.where(allowed, jnp.exp(scores - top[:, :, None]), 0.0)
        run_sum = run_sum + jnp.sum(weights, 2)
        run_acc = run_acc + jnp.einsum("hij,jhd->hid", weights, values_here)
    attended = (
        (run_acc / run_sum[:, :, None])
        .transpose(1, 0, 2)
        .reshape(dec_len, heads_here * HEAD_DIM)
        .astype(jnp.bfloat16)
    )

    feature_start = fsdp_index * feature_count
    gain_part = lax.dynamic_slice_in_dim(norm_gain, feature_start, feature_count, 0)
    hidden_part = lax.dynamic_slice_in_dim(dec_hidden, feature_start, feature_count, 1)
    if levels == 2:
        quarter = width // 4
        low_bit, high_bit = fsdp_index & 1, fsdp_index >> 1

        def chunk_product(chunk):
            columns = lax.dynamic_slice_in_dim(w_out, chunk * quarter, quarter, 1)
            return jnp.dot(attended, columns, preferred_element_type=jnp.float32)

        sent = jnp.stack([chunk_product(1 - low_bit), chunk_product(3 - low_bit)])
        kept = jnp.stack([chunk_product(low_bit), chunk_product(2 + low_bit)])
        kept = kept + exchange(sent, "fsdp", 0)
        mine = lax.dynamic_index_in_dim(kept, high_bit, 0, keepdims=False)
        other = lax.dynamic_index_in_dim(kept, 1 - high_bit, 0, keepdims=False)
        projected = mine + exchange(other.astype(jnp.bfloat16), "fsdp", 1).astype(jnp.float32)
    elif split_fsdp:
        projected = jnp.dot(attended, w_out, preferred_element_type=jnp.float32)
        projected = scatter_bits(projected, "fsdp", 1, levels, jnp.bfloat16)
    else:
        projected = jnp.dot(attended, w_out, preferred_element_type=jnp.float32)
        projected = lax.psum_scatter(projected, "fsdp", scatter_dimension=1, tiled=True)
    summed_part = projected + hidden_part.astype(jnp.float32)
    square_total = sum_all(jnp.sum(summed_part * summed_part, 1), "fsdp")
    inv_root = lax.rsqrt(square_total / width + 1e-06)
    unit_part = summed_part * inv_root[:, None]
    normed_part = (summed_part * gain_part).astype(jnp.bfloat16)
    if split_fsdp:
        half = width // 2
        top_side = (fsdp_index >> (levels - 1)) & 1
        near_rows = lax.dynamic_slice_in_dim(w_vocab, top_side * half, half, 0)
        far_rows = lax.dynamic_slice_in_dim(w_vocab, (1 - top_side) * half, half, 0)
        near_normed = gather_bits(normed_part, "fsdp", 1, levels - 1)
        far_normed = exchange(near_normed, "fsdp", levels - 1)
        logits = (
            jnp.dot(near_normed, near_rows, preferred_element_type=jnp.float32)
            + jnp.dot(far_normed, far_rows, preferred_element_type=jnp.float32)
        ) * inv_root[:, None]
    else:
        normed_full = lax.all_gather(normed_part, "fsdp", axis=1, tiled=True)
        logits = jnp.dot(normed_full, w_vocab, preferred_element_type=jnp.float32) * inv_root[:, None]
    local_target = targets - fsdp_index * vocab_here
    picked = jnp.arange(vocab_here)[None, :] == local_target[:, None]
    local_top = jnp.max(logits, 1)
    local_total = jnp.sum(jnp.exp(logits - local_top[:, None]), 1)
    local_pick = jnp.sum(jnp.where(picked, logits, 0.0), 1)
    row_top, row_total, target_logit = merge_all(
        jnp.stack([local_top, local_total, local_pick]), "fsdp"
    )
    log_total = row_top + jnp.log(row_total)
    mask_float = loss_mask.astype(jnp.float32)
    grad_logits = (
        mask_float[:, None] * (jnp.exp(logits - log_total[:, None]) - picked.astype(jnp.float32))
    ).astype(jnp.bfloat16)
    contract = (((1,), (1,)), ((), ()))
    if levels == 2:

        def grad_chunk(chunk, logits_in):
            rows_here = lax.dynamic_slice_in_dim(w_vocab, chunk * quarter, quarter, 0)
            return lax.dot_general(rows_here, logits_in, contract, preferred_element_type=jnp.float32)

        far_base = 2 * (1 - high_bit)
        far_kept = grad_chunk(far_base + low_bit, grad_logits) + exchange(
            grad_chunk(far_base + 1 - low_bit, grad_logits), "fsdp", 0
        )
        far_wire, rest_logits = lax.optimization_barrier(
            (far_kept.astype(jnp.bfloat16), grad_logits)
        )
        far_got = exchange(far_wire, "fsdp", 1).astype(jnp.float32)
        near_base = 2 * high_bit
        near_got = exchange(grad_chunk(near_base + 1 - low_bit, rest_logits), "fsdp", 0)
        own = grad_chunk(near_base + low_bit, rest_logits)
        grad_normed = (own + near_got + far_got).T
    elif split_fsdp:
        far_grad = lax.dot_general(
            far_rows, grad_logits, contract, preferred_element_type=jnp.float32
        )
        far_grad, near_logits = lax.optimization_barrier(
            (scatter_bits(far_grad, "fsdp", 0, levels - 1), grad_logits)
        )
        far_grad = exchange(far_grad.astype(jnp.bfloat16), "fsdp", levels - 1).astype(
            jnp.float32
        )
        near_grad = lax.dot_general(
            near_rows, near_logits, contract, preferred_element_type=jnp.float32
        )
        grad_normed = (scatter_bits(near_grad, "fsdp", 0, levels - 1) + far_grad).T
    else:
        grad_normed = lax.psum_scatter(
            lax.dot_general(w_vocab, grad_logits, contract, preferred_element_type=jnp.float32),
            "fsdp",
            scatter_dimension=0,
            tiled=True,
        ).T
    grad_unit = grad_normed * gain_part
    inner_total = sum_all(jnp.sum(grad_unit * unit_part, 1), "fsdp")
    grad_summed = inv_root[:, None] * (grad_unit - unit_part * (inner_total / width)[:, None])
    gain_local = jnp.sum(grad_normed * unit_part, 0)
    packed = jnp.concatenate(
        [jnp.stack([jnp.sum(mask_float), jnp.sum(mask_float * (log_total - target_logit))]), gain_local]
    )
    packed = sum_all(packed, "dp")
    token_count, loss_total, gain_total = packed[0], packed[1], packed[2:]
    return (
        loss_total / token_count,
        (grad_summed / token_count).astype(jnp.bfloat16),
        gain_total / token_count,
    )


def solution(mesh):
    in_specs = (
        P("dp", None),
        P(None, "fsdp"),
        P(None, "dp", "fsdp"),
        P("fsdp", None),
        P(),
        P(None, "fsdp"),
        P(),
        P("dp"),
        P(),
        P("dp"),
        P("dp"),
    )
    out_specs = (P(), P("dp", "fsdp"), P("fsdp"))
    return jax.shard_map(body, mesh=mesh, in_specs=in_specs, out_specs=out_specs, check_vma=False)
```

```python
import jax
import jax.numpy as jnp
from jax import lax
from jax.sharding import PartitionSpec as P

HEAD_DIM = 64
ENC_MOST = 80


def is_power_of_two(n):
    return n & (n - 1) == 0


def exchange(x, axis, bit):
    size = lax.axis_size(axis)
    return lax.ppermute(x, axis, [(i, i ^ (1 << bit)) for i in range(size)])


def scatter_bits(x, axis, dim, levels, last_wire=None):
    me = lax.axis_index(axis)
    chunks = 1 << levels
    head, width, tail = x.shape[:dim], x.shape[dim] // chunks, x.shape[dim + 1 :]
    cur = x
    bit = 0
    while chunks > 1:
        cur = cur.reshape(head + (chunks // 2, 2, width) + tail)
        side = (me >> bit) & 1
        keep = lax.dynamic_index_in_dim(cur, side, dim + 1, keepdims=False)
        send = lax.dynamic_index_in_dim(cur, 1 - side, dim + 1, keepdims=False)
        if last_wire is not None and chunks == 2:
            cur = keep + exchange(send.astype(last_wire), axis, bit).astype(keep.dtype)
        else:
            cur = keep + exchange(send, axis, bit)
        chunks //= 2
        bit += 1
    return cur.reshape(head + (width,) + tail)


def gather_bits(x, axis, dim, levels):
    me = lax.axis_index(axis)
    head, width, tail = x.shape[:dim], x.shape[dim], x.shape[dim + 1 :]
    cur = x.reshape(head + (1, width) + tail)
    chunks = 1
    for bit in range(levels):
        got = exchange(cur, axis, bit)
        low = (me >> bit) & 1 == 0
        first = jnp.where(low, cur, got)
        second = jnp.where(low, got, cur)
        cur = jnp.stack([first, second], dim).reshape(head + (chunks * 2, width) + tail)
        chunks *= 2
    return cur.reshape(head + (chunks * width,) + tail)


def sum_all(x, axis):
    size = lax.axis_size(axis)
    if not is_power_of_two(size):
        return lax.psum(x, axis)
    for bit in range(size.bit_length() - 1):
        x = x + exchange(x, axis, bit)
    return x


def merge_totals(first_set, second_set):
    larger = jnp.maximum(first_set[0], second_set[0])
    combined = first_set[1] * jnp.exp(first_set[0] - larger) + second_set[1] * jnp.exp(
        second_set[0] - larger
    )
    return jnp.stack([larger, combined, first_set[2] + second_set[2]])


def merge_all(stats, axis):
    size = lax.axis_size(axis)
    if is_power_of_two(size):
        for bit in range(size.bit_length() - 1):
            stats = merge_totals(stats, exchange(stats, axis, bit))
        return stats
    everything = lax.all_gather(stats, axis)
    return lax.fori_loop(1, size, lambda k, so_far: merge_totals(so_far, everything[k]), everything[0])


def body(
    dec_hidden,
    w_query,
    enc_states,
    w_out,
    norm_gain,
    w_vocab,
    enc_segment,
    dec_segment,
    seg_map,
    targets,
    loss_mask,
):
    dp_index = lax.axis_index("dp")
    fsdp_index = lax.axis_index("fsdp")
    dp_count = lax.axis_size("dp")
    fsdp_count = lax.axis_size("fsdp")
    dec_len, width = dec_hidden.shape
    enc_len = enc_states.shape[1]
    heads_here = w_query.shape[1] // HEAD_DIM
    segments = seg_map.shape[1]
    feature_count = width // fsdp_count
    vocab_here = w_vocab.shape[1]
    window = min(ENC_MOST, enc_len)
    split_fsdp = is_power_of_two(fsdp_count) and fsdp_count > 1
    levels = fsdp_count.bit_length() - 1

    rows = jnp.arange(dp_count)
    seg_ids = jnp.arange(segments)
    map_row = jnp.sum(jnp.where((rows == dp_index)[:, None], seg_map, 0), 0)
    sources = jnp.sum(
        jnp.where(dec_segment[:, None] == seg_ids[None, :], map_row[None, :], 0), 1
    )
    offsets = (seg_map[0] // segments) % dp_count
    hits = offsets[None, :] == rows[:, None]
    used = jnp.any(hits, 1)
    enc_rows = enc_segment.reshape(dp_count, enc_len)
    all_starts = jnp.sum(enc_rows[:, None, :] < seg_ids[None, :, None], 2)
    reader_hot = ((dp_index - rows) % dp_count)[:, None] == rows[None, :]
    reader_maps = jnp.sum(jnp.where(reader_hot[:, :, None], seg_map[None], 0), 1)
    send_seg = jnp.sum(jnp.where(hits, reader_maps, 0), 1) % segments
    my_starts = jnp.sum(jnp.where((rows == dp_index)[:, None], all_starts, 0), 0)
    send_start = jnp.clip(
        jnp.sum(jnp.where(send_seg[:, None] == seg_ids[None, :], my_starts[None, :], 0), 1),
        0,
        enc_len - window,
    )
    token_at = jnp.arange(enc_len)[None, None, :]
    send_pos = send_start[:, None] + jnp.arange(window)[None, :]
    pick = (token_at == send_pos[:, :, None]).astype(jnp.bfloat16)
    windows = jnp.einsum(
        "str,crf->sctf", pick, enc_states, preferred_element_type=jnp.float32
    ).astype(jnp.bfloat16)
    owner_hot = ((dp_index + rows) % dp_count)[:, None] == rows[None, :]
    owner_rows = jnp.sum(jnp.where(owner_hot[:, :, None], enc_rows[None], 0), 1)
    owner_starts = jnp.sum(jnp.where(owner_hot[:, :, None], all_starts[None], 0), 1)
    served = jnp.sum(jnp.where(hits, map_row[None, :], 0), 1)
    served_local = served % segments
    recv_start = jnp.clip(
        jnp.sum(jnp.where(served_local[:, None] == seg_ids[None, :], owner_starts, 0), 1),
        0,
        enc_len - window,
    )
    recv_pos = recv_start[:, None] + jnp.arange(window)[None, :]
    seg_at = jnp.sum(jnp.where(token_at == recv_pos[:, :, None], owner_rows[:, None, :], 0), 2)
    key_ids = jnp.where(used[:, None] & (seg_at == served_local[:, None]), served[:, None], -1)

    query_proj = jnp.dot(dec_hidden, w_query, preferred_element_type=jnp.float32).astype(
        jnp.bfloat16
    )
    queries = lax.optimization_barrier(query_proj).reshape(dec_len, heads_here, HEAD_DIM)
    run_sum = jnp.zeros((heads_here, dec_len), jnp.float32)
    run_acc = jnp.zeros((heads_here, dec_len, HEAD_DIM), jnp.float32)
    for shift in range(dp_count):
        block = windows[shift]
        if shift:
            block = lax.ppermute(
                block, "dp", [(i, (i - shift) % dp_count) for i in range(dp_count)]
            )
        keys_here = block[0].reshape(window, heads_here, HEAD_DIM)
        values_here = block[1].astype(jnp.float32).reshape(window, heads_here, HEAD_DIM)
        scores = jnp.einsum(
            "ihd,jhd->hij", queries, keys_here, preferred_element_type=jnp.float32
        )
        allowed = (sources[:, None] == key_ids[shift][None, :])[None]
        top = jnp.max(jnp.where(allowed, scores, jnp.float32(-1e30)), 2)
        weights = jnp.where(allowed, jnp.exp(scores - top[:, :, None]), 0.0)
        run_sum = run_sum + jnp.sum(weights, 2)
        run_acc = run_acc + jnp.einsum("hij,jhd->hid", weights, values_here)
    attended = (
        (run_acc / run_sum[:, :, None])
        .transpose(1, 0, 2)
        .reshape(dec_len, heads_here * HEAD_DIM)
        .astype(jnp.bfloat16)
    )

    feature_start = fsdp_index * feature_count
    gain_part = lax.dynamic_slice_in_dim(norm_gain, feature_start, feature_count, 0)
    hidden_part = lax.dynamic_slice_in_dim(dec_hidden, feature_start, feature_count, 1)
    if levels == 2:
        quarter = width // 4
        low_bit, high_bit = fsdp_index & 1, fsdp_index >> 1

        def chunk_product(chunk):
            columns = lax.dynamic_slice_in_dim(w_out, chunk * quarter, quarter, 1)
            return jnp.dot(attended, columns, preferred_element_type=jnp.float32)

        sent = jnp.stack([chunk_product(1 - low_bit), chunk_product(3 - low_bit)])
        kept = jnp.stack([chunk_product(low_bit), chunk_product(2 + low_bit)])
        kept = kept + exchange(sent, "fsdp", 0)
        mine = lax.dynamic_index_in_dim(kept, high_bit, 0, keepdims=False)
        other = lax.dynamic_index_in_dim(kept, 1 - high_bit, 0, keepdims=False)
        projected = mine + exchange(other.astype(jnp.bfloat16), "fsdp", 1).astype(jnp.float32)
    elif split_fsdp:
        projected = jnp.dot(attended, w_out, preferred_element_type=jnp.float32)
        projected = scatter_bits(projected, "fsdp", 1, levels, jnp.bfloat16)
    else:
        projected = jnp.dot(attended, w_out, preferred_element_type=jnp.float32)
        projected = lax.psum_scatter(projected, "fsdp", scatter_dimension=1, tiled=True)
    summed_part = projected + hidden_part.astype(jnp.float32)
    square_total = sum_all(jnp.sum(summed_part * summed_part, 1), "fsdp")
    inv_root = lax.rsqrt(square_total / width + 1e-06)
    unit_part = summed_part * inv_root[:, None]
    normed_part = (summed_part * gain_part).astype(jnp.bfloat16)
    if split_fsdp:
        half = width // 2
        top_side = (fsdp_index >> (levels - 1)) & 1
        near_rows = lax.dynamic_slice_in_dim(w_vocab, top_side * half, half, 0)
        far_rows = lax.dynamic_slice_in_dim(w_vocab, (1 - top_side) * half, half, 0)
        near_normed = gather_bits(normed_part, "fsdp", 1, levels - 1)
        far_normed = exchange(near_normed, "fsdp", levels - 1)
        logits = (
            jnp.dot(near_normed, near_rows, preferred_element_type=jnp.float32)
            + jnp.dot(far_normed, far_rows, preferred_element_type=jnp.float32)
        ) * inv_root[:, None]
    else:
        normed_full = lax.all_gather(normed_part, "fsdp", axis=1, tiled=True)
        logits = jnp.dot(normed_full, w_vocab, preferred_element_type=jnp.float32) * inv_root[:, None]
    local_target = targets - fsdp_index * vocab_here
    picked = jnp.arange(vocab_here)[None, :] == local_target[:, None]
    local_top = jnp.max(logits, 1)
    local_total = jnp.sum(jnp.exp(logits - local_top[:, None]), 1)
    local_pick = jnp.sum(jnp.where(picked, logits, 0.0), 1)
    row_top, row_total, target_logit = merge_all(
        jnp.stack([local_top, local_total, local_pick]), "fsdp"
    )
    log_total = row_top + jnp.log(row_total)
    mask_float = loss_mask.astype(jnp.float32)
    grad_logits = (
        mask_float[:, None] * (jnp.exp(logits - log_total[:, None]) - picked.astype(jnp.float32))
    ).astype(jnp.bfloat16)
    contract = (((1,), (1,)), ((), ()))
    if split_fsdp:
        far_grad = lax.dot_general(
            far_rows, grad_logits, contract, preferred_element_type=jnp.float32
        )
        far_grad = scatter_bits(far_grad, "fsdp", 0, levels - 1)
        near_logits = grad_logits
        far_grad = exchange(far_grad.astype(jnp.bfloat16), "fsdp", levels - 1).astype(
            jnp.float32
        )
        near_grad = lax.dot_general(
            near_rows, near_logits, contract, preferred_element_type=jnp.float32
        )
        grad_normed = (scatter_bits(near_grad, "fsdp", 0, levels - 1) + far_grad).T
    else:
        grad_normed = lax.psum_scatter(
            lax.dot_general(w_vocab, grad_logits, contract, preferred_element_type=jnp.float32),
            "fsdp",
            scatter_dimension=0,
            tiled=True,
        ).T
    grad_unit = grad_normed * gain_part
    inner_total = sum_all(jnp.sum(grad_unit * unit_part, 1), "fsdp")
    grad_summed = inv_root[:, None] * (grad_unit - unit_part * (inner_total / width)[:, None])
    gain_local = jnp.sum(grad_normed * unit_part, 0)
    packed = jnp.concatenate(
        [jnp.stack([jnp.sum(mask_float), jnp.sum(mask_float * (log_total - target_logit))]), gain_local]
    )
    packed = sum_all(packed, "dp")
    token_count, loss_total, gain_total = packed[0], packed[1], packed[2:]
    return (
        loss_total / token_count,
        (grad_summed / token_count).astype(jnp.bfloat16),
        gain_total / token_count,
    )


def solution(mesh):
    in_specs = (
        P("dp", None),
        P(None, "fsdp"),
        P(None, "dp", "fsdp"),
        P("fsdp", None),
        P(),
        P(None, "fsdp"),
        P(),
        P("dp"),
        P(),
        P("dp"),
        P("dp"),
    )
    out_specs = (P(), P("dp", "fsdp"), P("fsdp"))
    return jax.shard_map(body, mesh=mesh, in_specs=in_specs, out_specs=out_specs, check_vma=False)
```

```python
import jax
import jax.numpy as jnp
from jax import lax
from jax.sharding import PartitionSpec as P

HEAD_DIM = 64
ENC_MOST = 80


def is_power_of_two(n):
    return n & (n - 1) == 0


def exchange(x, axis, bit):
    size = lax.axis_size(axis)
    return lax.ppermute(x, axis, [(i, i ^ (1 << bit)) for i in range(size)])


def scatter_bits(x, axis, dim, levels, last_wire=None):
    me = lax.axis_index(axis)
    chunks = 1 << levels
    head, width, tail = x.shape[:dim], x.shape[dim] // chunks, x.shape[dim + 1 :]
    cur = x
    bit = 0
    while chunks > 1:
        cur = cur.reshape(head + (chunks // 2, 2, width) + tail)
        side = (me >> bit) & 1
        keep = lax.dynamic_index_in_dim(cur, side, dim + 1, keepdims=False)
        send = lax.dynamic_index_in_dim(cur, 1 - side, dim + 1, keepdims=False)
        if last_wire is not None and chunks == 2:
            cur = keep + exchange(send.astype(last_wire), axis, bit).astype(keep.dtype)
        else:
            cur = keep + exchange(send, axis, bit)
        chunks //= 2
        bit += 1
    return cur.reshape(head + (width,) + tail)


def gather_bits(x, axis, dim, levels):
    me = lax.axis_index(axis)
    head, width, tail = x.shape[:dim], x.shape[dim], x.shape[dim + 1 :]
    cur = x.reshape(head + (1, width) + tail)
    chunks = 1
    for bit in range(levels):
        got = exchange(cur, axis, bit)
        low = (me >> bit) & 1 == 0
        first = jnp.where(low, cur, got)
        second = jnp.where(low, got, cur)
        cur = jnp.stack([first, second], dim).reshape(head + (chunks * 2, width) + tail)
        chunks *= 2
    return cur.reshape(head + (chunks * width,) + tail)


def sum_all(x, axis):
    size = lax.axis_size(axis)
    if not is_power_of_two(size):
        return lax.psum(x, axis)
    for bit in range(size.bit_length() - 1):
        x = x + exchange(x, axis, bit)
    return x


def merge_totals(first_set, second_set):
    larger = jnp.maximum(first_set[0], second_set[0])
    combined = first_set[1] * jnp.exp(first_set[0] - larger) + second_set[1] * jnp.exp(
        second_set[0] - larger
    )
    return jnp.stack([larger, combined, first_set[2] + second_set[2]])


def merge_all(stats, axis):
    size = lax.axis_size(axis)
    if is_power_of_two(size):
        for bit in range(size.bit_length() - 1):
            stats = merge_totals(stats, exchange(stats, axis, bit))
        return stats
    everything = lax.all_gather(stats, axis)
    return lax.fori_loop(1, size, lambda k, so_far: merge_totals(so_far, everything[k]), everything[0])


def body(
    dec_hidden,
    w_query,
    enc_states,
    w_out,
    norm_gain,
    w_vocab,
    enc_segment,
    dec_segment,
    seg_map,
    targets,
    loss_mask,
):
    dp_index = lax.axis_index("dp")
    fsdp_index = lax.axis_index("fsdp")
    dp_count = lax.axis_size("dp")
    fsdp_count = lax.axis_size("fsdp")
    dec_len, width = dec_hidden.shape
    enc_len = enc_states.shape[1]
    heads_here = w_query.shape[1] // HEAD_DIM
    segments = seg_map.shape[1]
    feature_count = width // fsdp_count
    vocab_here = w_vocab.shape[1]
    window = min(ENC_MOST, enc_len)
    split_fsdp = is_power_of_two(fsdp_count) and fsdp_count > 1
    levels = fsdp_count.bit_length() - 1

    rows = jnp.arange(dp_count)
    seg_ids = jnp.arange(segments)
    map_row = jnp.sum(jnp.where((rows == dp_index)[:, None], seg_map, 0), 0)
    sources = jnp.sum(
        jnp.where(dec_segment[:, None] == seg_ids[None, :], map_row[None, :], 0), 1
    )
    offsets = (seg_map[0] // segments) % dp_count
    hits = offsets[None, :] == rows[:, None]
    used = jnp.any(hits, 1)
    enc_rows = enc_segment.reshape(dp_count, enc_len)
    all_starts = jnp.sum(enc_rows[:, None, :] < seg_ids[None, :, None], 2)
    reader_hot = ((dp_index - rows) % dp_count)[:, None] == rows[None, :]
    reader_maps = jnp.sum(jnp.where(reader_hot[:, :, None], seg_map[None], 0), 1)
    send_seg = jnp.sum(jnp.where(hits, reader_maps, 0), 1) % segments
    my_starts = jnp.sum(jnp.where((rows == dp_index)[:, None], all_starts, 0), 0)
    send_start = jnp.clip(
        jnp.sum(jnp.where(send_seg[:, None] == seg_ids[None, :], my_starts[None, :], 0), 1),
        0,
        enc_len - window,
    )
    token_at = jnp.arange(enc_len)[None, None, :]
    send_pos = send_start[:, None] + jnp.arange(window)[None, :]
    pick = (token_at == send_pos[:, :, None]).astype(jnp.bfloat16)
    windows = jnp.einsum(
        "str,crf->sctf", pick, enc_states, preferred_element_type=jnp.float32
    ).astype(jnp.bfloat16)
    owner_hot = ((dp_index + rows) % dp_count)[:, None] == rows[None, :]
    owner_rows = jnp.sum(jnp.where(owner_hot[:, :, None], enc_rows[None], 0), 1)
    owner_starts = jnp.sum(jnp.where(owner_hot[:, :, None], all_starts[None], 0), 1)
    served = jnp.sum(jnp.where(hits, map_row[None, :], 0), 1)
    served_local = served % segments
    recv_start = jnp.clip(
        jnp.sum(jnp.where(served_local[:, None] == seg_ids[None, :], owner_starts, 0), 1),
        0,
        enc_len - window,
    )
    recv_pos = recv_start[:, None] + jnp.arange(window)[None, :]
    seg_at = jnp.sum(jnp.where(token_at == recv_pos[:, :, None], owner_rows[:, None, :], 0), 2)
    key_ids = jnp.where(used[:, None] & (seg_at == served_local[:, None]), served[:, None], -1)

    query_proj = jnp.dot(dec_hidden, w_query, preferred_element_type=jnp.float32).astype(
        jnp.bfloat16
    )
    queries = lax.optimization_barrier(query_proj).reshape(dec_len, heads_here, HEAD_DIM)
    run_sum = jnp.zeros((heads_here, dec_len), jnp.float32)
    run_acc = jnp.zeros((heads_here, dec_len, HEAD_DIM), jnp.float32)
    for shift in range(dp_count):
        block = windows[shift]
        if shift:
            block = lax.ppermute(
                block, "dp", [(i, (i - shift) % dp_count) for i in range(dp_count)]
            )
        keys_here = block[0].reshape(window, heads_here, HEAD_DIM)
        values_here = block[1].astype(jnp.float32).reshape(window, heads_here, HEAD_DIM)
        scores = jnp.einsum(
            "ihd,jhd->hij", queries, keys_here, preferred_element_type=jnp.float32
        )
        allowed = (sources[:, None] == key_ids[shift][None, :])[None]
        top = jnp.max(jnp.where(allowed, scores, jnp.float32(-1e30)), 2)
        weights = jnp.where(allowed, jnp.exp(scores - top[:, :, None]), 0.0)
        run_sum = run_sum + jnp.sum(weights, 2)
        run_acc = run_acc + jnp.einsum("hij,jhd->hid", weights, values_here)
    attended = (
        (run_acc / run_sum[:, :, None])
        .transpose(1, 0, 2)
        .reshape(dec_len, heads_here * HEAD_DIM)
        .astype(jnp.bfloat16)
    )

    feature_start = fsdp_index * feature_count
    gain_part = lax.dynamic_slice_in_dim(norm_gain, feature_start, feature_count, 0)
    hidden_part = lax.dynamic_slice_in_dim(dec_hidden, feature_start, feature_count, 1)
    if levels == 2:
        quarter = width // 4
        low_bit, high_bit = fsdp_index & 1, fsdp_index >> 1

        def chunk_product(chunk):
            columns = lax.dynamic_slice_in_dim(w_out, chunk * quarter, quarter, 1)
            return jnp.dot(attended, columns, preferred_element_type=jnp.float32)

        sent = jnp.stack([chunk_product(1 - low_bit), chunk_product(3 - low_bit)])
        kept = jnp.stack([chunk_product(low_bit), chunk_product(2 + low_bit)])
        kept = kept + exchange(sent, "fsdp", 0)
        mine = lax.dynamic_index_in_dim(kept, high_bit, 0, keepdims=False)
        other = lax.dynamic_index_in_dim(kept, 1 - high_bit, 0, keepdims=False)
        projected = mine + exchange(other.astype(jnp.bfloat16), "fsdp", 1).astype(jnp.float32)
    elif split_fsdp:
        projected = jnp.dot(attended, w_out, preferred_element_type=jnp.float32)
        projected = scatter_bits(projected, "fsdp", 1, levels, jnp.bfloat16)
    else:
        projected = jnp.dot(attended, w_out, preferred_element_type=jnp.float32)
        projected = lax.psum_scatter(projected, "fsdp", scatter_dimension=1, tiled=True)
    summed_part = projected + hidden_part.astype(jnp.float32)
    square_total = sum_all(jnp.sum(summed_part * summed_part, 1), "fsdp")
    inv_root = lax.rsqrt(square_total / width + 1e-06)
    unit_part = summed_part * inv_root[:, None]
    normed_part = (summed_part * gain_part).astype(jnp.bfloat16)
    if split_fsdp:
        half = width // 2
        top_side = (fsdp_index >> (levels - 1)) & 1
        near_rows = lax.dynamic_slice_in_dim(w_vocab, top_side * half, half, 0)
        far_rows = lax.dynamic_slice_in_dim(w_vocab, (1 - top_side) * half, half, 0)
        if levels == 2:
            pair_normed = exchange(normed_part, "fsdp", 0)
            near_normed = jnp.where(
                low_bit == 0,
                jnp.concatenate([normed_part, pair_normed], 1),
                jnp.concatenate([pair_normed, normed_part], 1),
            )
        else:
            near_normed = gather_bits(normed_part, "fsdp", 1, levels - 1)
        far_normed = exchange(near_normed, "fsdp", levels - 1)
        logits = (
            jnp.dot(near_normed, near_rows, preferred_element_type=jnp.float32)
            + jnp.dot(far_normed, far_rows, preferred_element_type=jnp.float32)
        ) * inv_root[:, None]
    else:
        normed_full = lax.all_gather(normed_part, "fsdp", axis=1, tiled=True)
        logits = jnp.dot(normed_full, w_vocab, preferred_element_type=jnp.float32) * inv_root[:, None]
    local_target = targets - fsdp_index * vocab_here
    picked = jnp.arange(vocab_here)[None, :] == local_target[:, None]
    local_top = jnp.max(logits, 1)
    local_total = jnp.sum(jnp.exp(logits - local_top[:, None]), 1)
    local_pick = jnp.sum(jnp.where(picked, logits, 0.0), 1)
    row_top, row_total, target_logit = merge_all(
        jnp.stack([local_top, local_total, local_pick]), "fsdp"
    )
    log_total = row_top + jnp.log(row_total)
    mask_float = loss_mask.astype(jnp.float32)
    grad_logits = (
        mask_float[:, None] * (jnp.exp(logits - log_total[:, None]) - picked.astype(jnp.float32))
    ).astype(jnp.bfloat16)
    contract = (((1,), (1,)), ((), ()))
    if split_fsdp:
        far_grad = lax.dot_general(
            far_rows, grad_logits, contract, preferred_element_type=jnp.float32
        )
        far_grad = scatter_bits(far_grad, "fsdp", 0, levels - 1)
        near_logits = grad_logits
        far_grad = exchange(far_grad.astype(jnp.bfloat16), "fsdp", levels - 1).astype(
            jnp.float32
        )
        near_grad = lax.dot_general(
            near_rows, near_logits, contract, preferred_element_type=jnp.float32
        )
        grad_normed = (scatter_bits(near_grad, "fsdp", 0, levels - 1) + far_grad).T
    else:
        grad_normed = lax.psum_scatter(
            lax.dot_general(w_vocab, grad_logits, contract, preferred_element_type=jnp.float32),
            "fsdp",
            scatter_dimension=0,
            tiled=True,
        ).T
    grad_unit = grad_normed * gain_part
    inner_total = sum_all(jnp.sum(grad_unit * unit_part, 1), "fsdp")
    grad_summed = inv_root[:, None] * (grad_unit - unit_part * (inner_total / width)[:, None])
    gain_local = jnp.sum(grad_normed * unit_part, 0)
    packed = jnp.concatenate(
        [jnp.stack([jnp.sum(mask_float), jnp.sum(mask_float * (log_total - target_logit))]), gain_local]
    )
    packed = sum_all(packed, "dp")
    token_count, loss_total, gain_total = packed[0], packed[1], packed[2:]
    return (
        loss_total / token_count,
        (grad_summed / token_count).astype(jnp.bfloat16),
        gain_total / token_count,
    )


def solution(mesh):
    in_specs = (
        P("dp", None),
        P(None, "fsdp"),
        P(None, "dp", "fsdp"),
        P("fsdp", None),
        P(),
        P(None, "fsdp"),
        P(),
        P("dp"),
        P(),
        P("dp"),
        P("dp"),
    )
    out_specs = (P(), P("dp", "fsdp"), P("fsdp"))
    return jax.shard_map(body, mesh=mesh, in_specs=in_specs, out_specs=out_specs, check_vma=False)
```
